32 devices in a mesh: grid: 8 (over z, y), band: 4 (over x, core).
Axes of the slice: x: 2, y: 2, z: 4, core: 2. Of those that a mesh axis runs over, the one named last changes fastest.
Arguments:
- orbitals: float32 [2048, 512], P('grid', 'band'), may hold values from -30 to 30
- potential: float32 [2048], P('grid'), may hold values from -1 to 1
- fitted: bfloat16 [512, 2048], P('band', 'grid'), may hold values from -6 to 6
- points: int32 [512], P('grid'), may hold values from -1 to 255, as said below
Outputs:
- updated: float32 [2048, 512], P('grid', 'band')
The draws below stay inside these ranges and needn't reach their ends.
Inputs may be any that keep to these rules, and one draw needn't show every extreme that they name: Each block of 64 slots of one index of grid holds distinct grid points in its first slots and -1 in the rest; the numbers of filled slots of blocks 2i and 2i + 1 sum to 64, so that 256 slots are filled in all, and some block is full.
All inputs are finite; a program needn't handle non-finite values.
Results may differ from the reference program's by a relative error of at most 0.024.
Values may be sent and summed in bfloat16 or wider, within the bound.
No kernel may reach another device: no remote copies, remote signals or barrier semaphores. Data moves between devices by JAX's collectives and lax.ppermute only.
A program may use at most 64 MiB of HBM per device.

```python
import math
import jax
import jax.numpy as jnp
from jax import lax

ORBITAL_COUNT = 512
GRID_ROWS = 256
CAP = 64
ITERS = 2
NG = 2048
INTERP_SLOTS = 512
N_GRID = 8
N_BAND = 4


def draw_orbitals(key, part):
    first, second = jax.random.split(key, 2)
    where_row = jnp.arange(NG, dtype=jnp.float32) / NG
    rising = jnp.exp(math.log(3.0) * where_row)[:, None]
    base = jnp.clip(jax.random.normal(first, (NG, ORBITAL_COUNT), jnp.float32), -5.5, 5.5)
    rough = jnp.exp(jax.random.uniform(second, (NG, 1), jnp.float32, 0.0, math.log(1.5)))
    return base * rising * rough * 1.2


def draw_points(key, part):
    shards = INTERP_SLOTS // CAP
    first, second, third, fourth = jax.random.split(key, 4)
    heavy = CAP - jax.random.randint(first, (shards // 2,), 0, CAP // 4 + 1)
    chosen = jax.random.randint(third, (), 0, shards // 2)
    heavy = heavy.at[chosen].set(CAP)
    flip = jax.random.randint(fourth, (shards // 2,), 0, 2)
    leading = jnp.where(flip == 1, CAP - heavy, heavy)
    counts = jnp.stack([leading, CAP - leading], axis=1).reshape(shards)
    keys = jax.random.split(second, shards)
    picked = jax.vmap(lambda one: jax.random.permutation(one, GRID_ROWS)[:CAP])(keys).astype(jnp.int32)
    live = jnp.arange(CAP, dtype=jnp.int32)[None, :] < counts[:, None]
    return jnp.where(live, picked, -1).reshape(INTERP_SLOTS).astype(jnp.int32)


def level_of(own_key, shape, cuts, smallest, high):
    def one(position, parts):
        draws = jax.random.uniform(jax.random.fold_in(jax.random.fold_in(own_key, 6), position), (parts,), jnp.float32, smallest / len(cuts), high / len(cuts))
        return jnp.repeat(jnp.exp(draws), shape[position] // parts).reshape((-1,) + (1,) * (len(shape) - position - 1))

    factor_of = one(*cuts[0])
    for cut in cuts[1:]:
        factor_of = factor_of * one(*cut)
    return factor_of


def noise(own_key, shape, deviation, most, pieces=(), held_as=jnp.bfloat16):
    drawn = deviation * jax.random.normal(own_key, shape, jnp.float32)
    if pieces:
        drawn = drawn * level_of(own_key, shape, pieces, -0.22, 0.18)
    return jnp.clip(drawn, -most, most).astype(held_as)


def setup_inputs(seed: int = 0) -> dict:
    key_of = jax.random.split(jax.random.key(seed), 5)
    return {
        "orbitals": draw_orbitals(jax.random.fold_in(key_of[4], 71), 0),
        "potential": jnp.clip(jax.random.uniform(key_of[1], (NG,), jnp.float32, -1.0, 1.0) * level_of(key_of[1], (NG,), ((0, 8),), -0.4, 0.0), -1.0, 1.0),
        "fitted": noise(key_of[2], (INTERP_SLOTS, NG), 1.0, 6.0, ((0, 4), (1, 8))),
        "points": draw_points(jax.random.fold_in(key_of[4], 71), 0),
    }


def reference(orbitals, potential, fitted, points):
    valid_mask = points >= 0
    block_ids = (jnp.arange(INTERP_SLOTS, dtype=jnp.int32) // CAP).astype(jnp.int32)
    global_index = jnp.where(valid_mask, points + block_ids * GRID_ROWS, 0).astype(jnp.int32)
    block_width = ORBITAL_COUNT // N_BAND
    fitted_blocks = fitted.reshape(INTERP_SLOTS, N_GRID, GRID_ROWS).transpose(1, 0, 2)
    psi = orbitals
    for step in range(ITERS):
        orbital_block = psi.astype(jnp.bfloat16)
        collocation_matrix = jnp.where(valid_mask[:, None], orbital_block[global_index], jnp.zeros((), jnp.bfloat16))
        collocation_triple = collocation_matrix.reshape(INTERP_SLOTS, N_BAND, block_width).astype(jnp.float32)

        def apply_block(pair):
            block_rows, w_blk = pair
            partition_count = jnp.einsum('zax,max->azm', collocation_triple, block_rows.reshape(GRID_ROWS, N_BAND, block_width).astype(jnp.float32)) / ORBITAL_COUNT
            partition_count = lax.optimization_barrier(partition_count.astype(jnp.bfloat16))
            proj = lax.optimization_barrier(jnp.sum(partition_count.astype(jnp.float32), axis=0))
            tile_blocks = (w_blk.astype(jnp.float32) * proj).astype(jnp.bfloat16)
            return jnp.dot(tile_blocks.T, collocation_matrix, preferred_element_type=jnp.float32)
        applied = lax.map(apply_block, (orbital_block.reshape(N_GRID, GRID_ROWS, ORBITAL_COUNT), fitted_blocks)).reshape(NG, ORBITAL_COUNT)
        fresh = psi - 0.25 * (potential[:, None] * psi - applied)
        psi = fresh * lax.rsqrt(lax.optimization_barrier(jnp.mean(fresh * fresh, axis=0)) + 1e-06)
    return psi
```

```python
import jax
import jax.numpy as jnp
from jax import lax
from jax.sharding import PartitionSpec as P

ITERS = 2


def grid_gather(x):
    ngroups = lax.axis_size("grid")
    sent = jnp.broadcast_to(x[None], (ngroups,) + x.shape)
    got = lax.all_to_all(sent, "grid", 0, 0, tiled=True)
    return got.reshape((ngroups * x.shape[0],) + x.shape[1:])


def band_gather(x, axis):
    return lax.all_gather(x, "band", axis=axis, tiled=True)


def body(orbitals, potential, fitted, points):
    if lax.axis_size("grid") > 8:
        return body_spread(orbitals, potential, fitted, points)
    rows = orbitals.shape[0]
    block_width = orbitals.shape[1]
    nbands = lax.axis_size("band")
    ngroups = lax.axis_size("grid")
    band = lax.axis_index("band")
    total_orbitals = block_width * nbands
    valid_mask = points >= 0
    safe_idx = jnp.where(valid_mask, points, 0)
    psi = band_gather(orbitals, 1)
    fitted_all = band_gather(fitted, 0).astype(jnp.float32)
    pot = potential[:, None]
    scale = None
    for step in range(ITERS):
        if scale is None:
            orbital_block = psi.astype(jnp.bfloat16)
            selected = jnp.where(valid_mask[:, None], orbital_block[safe_idx], jnp.zeros((), jnp.bfloat16))
            coll = grid_gather(selected)
        else:
            at_slots = jnp.where(valid_mask[:, None], psi[safe_idx], 0.0)
            got = grid_gather(jnp.concatenate([at_slots, sq[None]], 0)).reshape(ngroups, -1, total_orbitals)
            total = jnp.sum(got[:, -1], axis=0)
            scale = lax.rsqrt(total / (rows * ngroups) + 1e-06)
            psi = psi * scale
            orbital_block = psi.astype(jnp.bfloat16)
            coll = (got[:, :-1] * scale).astype(jnp.bfloat16).reshape(-1, total_orbitals)
        proj = None
        for k in range(nbands):
            part = lax.dot_general(
                coll[:, k * block_width:(k + 1) * block_width],
                orbital_block[:, k * block_width:(k + 1) * block_width],
                (((1,), (1,)), ((), ())),
                preferred_element_type=jnp.float32,
            )
            part = (part / total_orbitals).astype(jnp.bfloat16).astype(jnp.float32)
            proj = part if proj is None else proj + part
        tile_blocks = (fitted_all * proj).astype(jnp.bfloat16)
        applied = lax.dot_general(
            tile_blocks, coll, (((0,), (0,)), ((), ())), preferred_element_type=jnp.float32
        )
        psi = psi - 0.25 * (pot * psi - applied)
        sq = jnp.sum(psi * psi, axis=0)
        scale = sq
    mine = lax.dynamic_slice_in_dim(psi, band * block_width, block_width, axis=1)
    mine_sq = lax.dynamic_slice_in_dim(sq, band * block_width, block_width)
    total = jnp.sum(grid_gather(mine_sq[None]), axis=0)
    return mine * lax.rsqrt(total / (rows * ngroups) + 1e-06)


def body_spread(orbitals, potential, fitted, points):
    rows = orbitals.shape[0]
    block_width = orbitals.shape[1]
    nbands = lax.axis_size("band")
    ngroups = lax.axis_size("grid")
    total_orbitals = block_width * nbands
    valid_mask = points >= 0
    safe_idx = jnp.where(valid_mask, points, 0)
    psi = orbitals
    for step in range(ITERS):
        orbital_block = psi.astype(jnp.bfloat16)
        selected_points = jnp.where(
            valid_mask[:, None], orbital_block[safe_idx], jnp.zeros((), jnp.bfloat16)
        )
        collocation_matrix = lax.all_gather(selected_points, "grid", axis=0, tiled=True)
        product = lax.dot_general(
            collocation_matrix,
            orbital_block,
            (((1,), (1,)), ((), ())),
            preferred_element_type=jnp.float32,
        )
        proj = lax.psum_scatter(
            (product / total_orbitals).astype(jnp.bfloat16), "band", scatter_dimension=0, tiled=True
        ).astype(jnp.float32)
        tile_blocks = (fitted.astype(jnp.float32) * proj).astype(jnp.bfloat16)
        orbitals_at_slots = lax.all_to_all(
            collocation_matrix, "band", split_axis=0, concat_axis=1, tiled=True
        )
        partial_value = lax.dot_general(
            tile_blocks,
            orbitals_at_slots,
            (((0,), (0,)), ((), ())),
            preferred_element_type=jnp.float32,
        )
        applied = lax.psum_scatter(
            partial_value.astype(jnp.bfloat16), "band", scatter_dimension=1, tiled=True
        ).astype(jnp.float32)
        fresh = psi - 0.25 * (potential[:, None] * psi - applied)
        squares = lax.psum(jnp.sum(fresh * fresh, axis=0), "grid")
        psi = fresh * lax.rsqrt(squares / (rows * ngroups) + 1e-06)
    return psi


def solution(mesh):
    in_specs = (P("grid", "band"), P("grid"), P("band", "grid"), P("grid"))
    out_specs = P("grid", "band")
    return jax.shard_map(body, mesh=mesh, in_specs=in_specs, out_specs=out_specs, check_vma=False)
```

```python
import jax
import jax.numpy as jnp
from jax import lax
from jax.sharding import PartitionSpec as P

ITERS = 2


def grid_gather(x):
    ngroups = lax.axis_size("grid")
    sent = jnp.broadcast_to(x[None], (ngroups,) + x.shape)
    got = lax.all_to_all(sent, "grid", 0, 0, tiled=True)
    return got.reshape((ngroups * x.shape[0],) + x.shape[1:])


def band_gather(x, axis):
    return lax.all_gather(x, "band", axis=axis, tiled=True)


def body(orbitals, potential, fitted, points):
    if lax.axis_size("grid") > 8:
        return body_spread(orbitals, potential, fitted, points)
    rows = orbitals.shape[0]
    block_width = orbitals.shape[1]
    nbands = lax.axis_size("band")
    ngroups = lax.axis_size("grid")
    band = lax.axis_index("band")
    total_orbitals = block_width * nbands
    valid_mask = points >= 0
    safe_idx = jnp.where(valid_mask, points, 0)
    psi = band_gather(orbitals, 1)
    fitted_all = band_gather(fitted, 0).astype(jnp.float32)
    pot = potential[:, None]
    scale = None
    for step in range(ITERS):
        if scale is None:
            orbital_block = psi.astype(jnp.bfloat16)
            selected = jnp.where(valid_mask[:, None], orbital_block[safe_idx], jnp.zeros((), jnp.bfloat16))
            coll = grid_gather(selected)
        else:
            own = lax.dynamic_slice_in_dim(psi, band * block_width, block_width, axis=1)
            at_slots = jnp.where(valid_mask[:, None], own[safe_idx], 0.0)
            nslots = at_slots.shape[0]
            payload = jnp.concatenate([at_slots, sq.reshape(nbands, block_width)], 0)
            got = grid_gather(payload).reshape(ngroups, nslots + nbands, block_width)
            total = jnp.sum(got[:, nslots:], axis=0).reshape(total_orbitals)
            scale = lax.rsqrt(total / (rows * ngroups) + 1e-06)
            own_scale = lax.dynamic_slice_in_dim(scale, band * block_width, block_width)
            coll_own = (got[:, :nslots] * own_scale).astype(jnp.bfloat16).reshape(-1, block_width)
            coll = band_gather(coll_own, 1)
            psi = psi * scale
            orbital_block = psi.astype(jnp.bfloat16)
        proj = None
        for k in range(nbands):
            part = lax.dot_general(
                coll[:, k * block_width:(k + 1) * block_width],
                orbital_block[:, k * block_width:(k + 1) * block_width],
                (((1,), (1,)), ((), ())),
                preferred_element_type=jnp.float32,
            )
            part = (part / total_orbitals).astype(jnp.bfloat16).astype(jnp.float32)
            proj = part if proj is None else proj + part
        tile_blocks = (fitted_all * proj).astype(jnp.bfloat16)
        applied = lax.dot_general(
            tile_blocks, coll, (((0,), (0,)), ((), ())), preferred_element_type=jnp.float32
        )
        psi = psi - 0.25 * (pot * psi - applied)
        sq = jnp.sum(psi * psi, axis=0)
        scale = sq
    mine = lax.dynamic_slice_in_dim(psi, band * block_width, block_width, axis=1)
    mine_sq = lax.dynamic_slice_in_dim(sq, band * block_width, block_width)
    total = jnp.sum(grid_gather(mine_sq[None]), axis=0)
    return mine * lax.rsqrt(total / (rows * ngroups) + 1e-06)


def body_spread(orbitals, potential, fitted, points):
    rows = orbitals.shape[0]
    block_width = orbitals.shape[1]
    nbands = lax.axis_size("band")
    ngroups = lax.axis_size("grid")
    total_orbitals = block_width * nbands
    valid_mask = points >= 0
    safe_idx = jnp.where(valid_mask, points, 0)
    psi = orbitals
    for step in range(ITERS):
        orbital_block = psi.astype(jnp.bfloat16)
        selected_points = jnp.where(
            valid_mask[:, None], orbital_block[safe_idx], jnp.zeros((), jnp.bfloat16)
        )
        collocation_matrix = lax.all_gather(selected_points, "grid", axis=0, tiled=True)
        product = lax.dot_general(
            collocation_matrix,
            orbital_block,
            (((1,), (1,)), ((), ())),
            preferred_element_type=jnp.float32,
        )
        proj = lax.psum_scatter(
            (product / total_orbitals).astype(jnp.bfloat16), "band", scatter_dimension=0, tiled=True
        ).astype(jnp.float32)
        tile_blocks = (fitted.astype(jnp.float32) * proj).astype(jnp.bfloat16)
        orbitals_at_slots = lax.all_to_all(
            collocation_matrix, "band", split_axis=0, concat_axis=1, tiled=True
        )
        partial_value = lax.dot_general(
            tile_blocks,
            orbitals_at_slots,
            (((0,), (0,)), ((), ())),
            preferred_element_type=jnp.float32,
        )
        applied = lax.psum_scatter(
            partial_value.astype(jnp.bfloat16), "band", scatter_dimension=1, tiled=True
        ).astype(jnp.float32)
        fresh = psi - 0.25 * (potential[:, None] * psi - applied)
        squares = lax.psum(jnp.sum(fresh * fresh, axis=0), "grid")
        psi = fresh * lax.rsqrt(squares / (rows * ngroups) + 1e-06)
    return psi


def solution(mesh):
    in_specs = (P("grid", "band"), P("grid"), P("band", "grid"), P("grid"))
    out_specs = P("grid", "band")
    return jax.shard_map(body, mesh=mesh, in_specs=in_specs, out_specs=out_specs, check_vma=False)
```

```python
import jax
import jax.numpy as jnp
from jax import lax
from jax.sharding import PartitionSpec as P

ITERS = 2


def grid_gather(x):
    ngroups = lax.axis_size("grid")
    sent = jnp.broadcast_to(x[None], (ngroups,) + x.shape)
    got = lax.all_to_all(sent, "grid", 0, 0, tiled=True)
    return got.reshape((ngroups * x.shape[0],) + x.shape[1:])


def band_swap(x):
    nbands = lax.axis_size("band")
    got = [x]
    for k in range(1, nbands):
        got.append(lax.ppermute(x, "band", [(i, i ^ k) for i in range(nbands)]))
    return got


def body(orbitals, potential, fitted, points):
    if lax.axis_size("grid") > 8:
        return body_spread(orbitals, potential, fitted, points)
    rows = orbitals.shape[0]
    block_width = orbitals.shape[1]
    nbands = lax.axis_size("band")
    ngroups = lax.axis_size("grid")
    band = lax.axis_index("band")
    total_orbitals = block_width * nbands
    valid_mask = points >= 0
    safe_idx = jnp.where(valid_mask, points, 0)
    psi = jnp.concatenate(band_swap(orbitals), 1)
    fitted_got = jnp.stack(band_swap(fitted), 0)
    fitted_all = jnp.take(fitted_got, jnp.arange(nbands, dtype=jnp.int32) ^ band, axis=0)
    fitted_all = fitted_all.reshape(-1, fitted.shape[1]).astype(jnp.float32)
    pot = potential[:, None]
    sq = None
    for step in range(ITERS):
        if sq is None:
            own_b = orbitals.astype(jnp.bfloat16)
            selected = jnp.where(valid_mask[:, None], own_b[safe_idx], jnp.zeros((), jnp.bfloat16))
            coll = jnp.concatenate(band_swap(grid_gather(selected)), 1)
            orbital_block = psi.astype(jnp.bfloat16)
        else:
            own = psi[:, :block_width]
            at_slots = jnp.where(valid_mask[:, None], own[safe_idx], 0.0)
            nslots = at_slots.shape[0]
            payload = jnp.concatenate([at_slots, sq.reshape(nbands, block_width)], 0)
            got = grid_gather(payload).reshape(ngroups, nslots + nbands, block_width)
            total = jnp.sum(got[:, nslots:], axis=0).reshape(total_orbitals)
            scale = lax.rsqrt(total / (rows * ngroups) + 1e-06)
            coll_own = (got[:, :nslots] * scale[:block_width]).astype(jnp.bfloat16).reshape(-1, block_width)
            coll = jnp.concatenate(band_swap(coll_own), 1)
            psi = psi * scale
            orbital_block = psi.astype(jnp.bfloat16)
        proj = None
        for k in range(nbands):
            part = lax.dot_general(
                coll[:, k * block_width:(k + 1) * block_width],
                orbital_block[:, k * block_width:(k + 1) * block_width],
                (((1,), (1,)), ((), ())),
                preferred_element_type=jnp.float32,
            )
            part = (part / total_orbitals).astype(jnp.bfloat16).astype(jnp.float32)
            proj = part if proj is None else proj + part
        tile_blocks = (fitted_all * proj).astype(jnp.bfloat16)
        applied = lax.dot_general(
            tile_blocks, coll, (((0,), (0,)), ((), ())), preferred_element_type=jnp.float32
        )
        psi = psi - 0.25 * (pot * psi - applied)
        sq = jnp.sum(psi * psi, axis=0)
    total = jnp.sum(grid_gather(sq[None, :block_width]), axis=0)
    return psi[:, :block_width] * lax.rsqrt(total / (rows * ngroups) + 1e-06)


def body_spread(orbitals, potential, fitted, points):
    rows = orbitals.shape[0]
    block_width = orbitals.shape[1]
    nbands = lax.axis_size("band")
    ngroups = lax.axis_size("grid")
    total_orbitals = block_width * nbands
    valid_mask = points >= 0
    safe_idx = jnp.where(valid_mask, points, 0)
    psi = orbitals
    for step in range(ITERS):
        orbital_block = psi.astype(jnp.bfloat16)
        selected_points = jnp.where(
            valid_mask[:, None], orbital_block[safe_idx], jnp.zeros((), jnp.bfloat16)
        )
        collocation_matrix = lax.all_gather(selected_points, "grid", axis=0, tiled=True)
        product = lax.dot_general(
            collocation_matrix,
            orbital_block,
            (((1,), (1,)), ((), ())),
            preferred_element_type=jnp.float32,
        )
        proj = lax.psum_scatter(
            (product / total_orbitals).astype(jnp.bfloat16), "band", scatter_dimension=0, tiled=True
        ).astype(jnp.float32)
        tile_blocks = (fitted.astype(jnp.float32) * proj).astype(jnp.bfloat16)
        orbitals_at_slots = lax.all_to_all(
            collocation_matrix, "band", split_axis=0, concat_axis=1, tiled=True
        )
        partial_value = lax.dot_general(
            tile_blocks,
            orbitals_at_slots,
            (((0,), (0,)), ((), ())),
            preferred_element_type=jnp.float32,
        )
        applied = lax.psum_scatter(
            partial_value.astype(jnp.bfloat16), "band", scatter_dimension=1, tiled=True
        ).astype(jnp.float32)
        fresh = psi - 0.25 * (potential[:, None] * psi - applied)
        squares = lax.psum(jnp.sum(fresh * fresh, axis=0), "grid")
        psi = fresh * lax.rsqrt(squares / (rows * ngroups) + 1e-06)
    return psi


def solution(mesh):
    in_specs = (P("grid", "band"), P("grid"), P("band", "grid"), P("grid"))
    out_specs = P("grid", "band")
    return jax.shard_map(body, mesh=mesh, in_specs=in_specs, out_specs=out_specs, check_vma=False)
```

```python
import jax
import jax.numpy as jnp
from jax import lax
from jax.sharding import PartitionSpec as P

ITERS = 2


def grid_gather(x):
    ngroups = lax.axis_size("grid")
    sent = jnp.broadcast_to(x[None], (ngroups,) + x.shape)
    got = lax.all_to_all(sent, "grid", 0, 0, tiled=True)
    return got.reshape((ngroups * x.shape[0],) + x.shape[1:])


def band_swap(x):
    nbands = lax.axis_size("band")
    got = [x]
    for k in range(1, nbands):
        got.append(lax.ppermute(x, "band", [(i, i ^ k) for i in range(nbands)]))
    return got


def pair_up(slots):
    ngroups, nslots = slots.shape[:2]
    pairs = slots.reshape((ngroups // 2, 2) + slots.shape[1:])
    return (pairs[:, 0] + jnp.flip(pairs[:, 1], axis=1)).reshape((ngroups // 2 * nslots,) + slots.shape[2:])


def body(orbitals, potential, fitted, points):
    if lax.axis_size("grid") > 8 or lax.axis_size("grid") % 2 or points.shape[0] > orbitals.shape[1]:
        return body_spread(orbitals, potential, fitted, points)
    rows = orbitals.shape[0]
    block_width = orbitals.shape[1]
    nbands = lax.axis_size("band")
    ngroups = lax.axis_size("grid")
    band = lax.axis_index("band")
    total_orbitals = block_width * nbands
    valid_mask = points >= 0
    safe_idx = jnp.where(valid_mask, points, 0)
    psi = jnp.concatenate(band_swap(orbitals), 1)
    fitted_got = jnp.stack(band_swap(fitted), 0)
    fitted_all = jnp.take(fitted_got, jnp.arange(nbands, dtype=jnp.int32) ^ band, axis=0)
    fitted_all = fitted_all.reshape(ngroups // 2, 2, points.shape[0], fitted.shape[1])
    pot = potential[:, None]
    sq = None
    for step in range(ITERS):
        if sq is None:
            own_b = orbitals.astype(jnp.bfloat16)
            nslots = points.shape[0]
            selected = jnp.where(valid_mask[:, None], own_b[safe_idx], jnp.zeros((), jnp.bfloat16))
            filled = jnp.pad(valid_mask.astype(jnp.bfloat16), (0, block_width - nslots))
            got = grid_gather(jnp.concatenate([selected, filled[None]], 0)).reshape(ngroups, nslots + 1, block_width)
            coll = jnp.concatenate(band_swap(pair_up(got[:, :nslots])), 1)
            first_filled = got[:, nslots, :nslots].reshape(ngroups // 2, 2, nslots)[:, 0] > 0
            fitted_all = jnp.where(
                first_filled[:, :, None], fitted_all[:, 0], jnp.flip(fitted_all[:, 1], axis=1)
            ).reshape(-1, fitted.shape[1]).astype(jnp.float32)
            orbital_block = psi.astype(jnp.bfloat16)
        else:
            own = psi[:, :block_width]
            at_slots = jnp.where(valid_mask[:, None], own[safe_idx], 0.0)
            nslots = at_slots.shape[0]
            payload = jnp.concatenate([at_slots, sq.reshape(nbands, block_width)], 0)
            got = grid_gather(payload).reshape(ngroups, nslots + nbands, block_width)
            total = jnp.sum(got[:, nslots:], axis=0).reshape(total_orbitals)
            scale = lax.rsqrt(total / (rows * ngroups) + 1e-06)
            coll_own = pair_up((got[:, :nslots] * scale[:block_width]).astype(jnp.bfloat16))
            coll = jnp.concatenate(band_swap(coll_own), 1)
            psi = psi * scale
            orbital_block = psi.astype(jnp.bfloat16)
        proj = None
        for k in range(nbands):
            part = lax.dot_general(
                coll[:, k * block_width:(k + 1) * block_width],
                orbital_block[:, k * block_width:(k + 1) * block_width],
                (((1,), (1,)), ((), ())),
                preferred_element_type=jnp.float32,
            )
            part = (part / total_orbitals).astype(jnp.bfloat16).astype(jnp.float32)
            proj = part if proj is None else proj + part
        tile_blocks = (fitted_all * proj).astype(jnp.bfloat16)
        applied = lax.dot_general(
            tile_blocks, coll, (((0,), (0,)), ((), ())), preferred_element_type=jnp.float32
        )
        psi = psi - 0.25 * (pot * psi - applied)
        sq = jnp.sum(psi * psi, axis=0)
    total = jnp.sum(grid_gather(sq[None, :block_width]), axis=0)
    return psi[:, :block_width] * lax.rsqrt(total / (rows * ngroups) + 1e-06)


def body_spread(orbitals, potential, fitted, points):
    rows = orbitals.shape[0]
    block_width = orbitals.shape[1]
    nbands = lax.axis_size("band")
    ngroups = lax.axis_size("grid")
    total_orbitals = block_width * nbands
    valid_mask = points >= 0
    safe_idx = jnp.where(valid_mask, points, 0)
    psi = orbitals
    for step in range(ITERS):
        orbital_block = psi.astype(jnp.bfloat16)
        selected_points = jnp.where(
            valid_mask[:, None], orbital_block[safe_idx], jnp.zeros((), jnp.bfloat16)
        )
        collocation_matrix = lax.all_gather(selected_points, "grid", axis=0, tiled=True)
        product = lax.dot_general(
            collocation_matrix,
            orbital_block,
            (((1,), (1,)), ((), ())),
            preferred_element_type=jnp.float32,
        )
        proj = lax.psum_scatter(
            (product / total_orbitals).astype(jnp.bfloat16), "band", scatter_dimension=0, tiled=True
        ).astype(jnp.float32)
        tile_blocks = (fitted.astype(jnp.float32) * proj).astype(jnp.bfloat16)
        orbitals_at_slots = lax.all_to_all(
            collocation_matrix, "band", split_axis=0, concat_axis=1, tiled=True
        )
        partial_value = lax.dot_general(
            tile_blocks,
            orbitals_at_slots,
            (((0,), (0,)), ((), ())),
            preferred_element_type=jnp.float32,
        )
        applied = lax.psum_scatter(
            partial_value.astype(jnp.bfloat16), "band", scatter_dimension=1, tiled=True
        ).astype(jnp.float32)
        fresh = psi - 0.25 * (potential[:, None] * psi - applied)
        squares = lax.psum(jnp.sum(fresh * fresh, axis=0), "grid")
        psi = fresh * lax.rsqrt(squares / (rows * ngroups) + 1e-06)
    return psi


def solution(mesh):
    in_specs = (P("grid", "band"), P("grid"), P("band", "grid"), P("grid"))
    out_specs = P("grid", "band")
    return jax.shard_map(body, mesh=mesh, in_specs=in_specs, out_specs=out_specs, check_vma=False)
```

```python
import jax
import jax.numpy as jnp
from jax import lax
from jax.sharding import PartitionSpec as P

ITERS = 2


def grid_copies(x):
    ngroups = lax.axis_size("grid")
    return jnp.broadcast_to(x[None], (ngroups,) + x.shape)


def grid_exchange(sent):
    got = lax.all_to_all(sent, "grid", 0, 0, tiled=True)
    return got.reshape((sent.shape[0] * sent.shape[1],) + sent.shape[2:])


def grid_gather(x):
    return grid_exchange(grid_copies(x))


def band_swap(x):
    nbands = lax.axis_size("band")
    got = [x]
    for k in range(1, nbands):
        got.append(lax.ppermute(x, "band", [(i, i ^ k) for i in range(nbands)]))
    return got


def pair_up(slots):
    ngroups, nslots = slots.shape[:2]
    pairs = slots.reshape((ngroups // 2, 2) + slots.shape[1:])
    return (pairs[:, 0] + jnp.flip(pairs[:, 1], axis=1)).reshape((ngroups // 2 * nslots,) + slots.shape[2:])


def body(orbitals, potential, fitted, points):
    if lax.axis_size("grid") > 8 or lax.axis_size("grid") % 2 or points.shape[0] > orbitals.shape[1]:
        return body_spread(orbitals, potential, fitted, points)
    rows = orbitals.shape[0]
    block_width = orbitals.shape[1]
    nbands = lax.axis_size("band")
    ngroups = lax.axis_size("grid")
    band = lax.axis_index("band")
    total_orbitals = block_width * nbands
    valid_mask = points >= 0
    safe_idx = jnp.where(valid_mask, points, 0)
    pot = potential[:, None]
    sq = None
    for step in range(ITERS):
        if sq is None:
            own_b = orbitals.astype(jnp.bfloat16)
            nslots = points.shape[0]
            selected = jnp.where(valid_mask[:, None], own_b[safe_idx], jnp.zeros((), jnp.bfloat16))
            filled = jnp.pad(valid_mask.astype(jnp.bfloat16), (0, block_width - nslots))
            payload = jnp.concatenate([selected, filled[None]], 0)
            sent, rows_own, fitted_own = lax.optimization_barrier((grid_copies(payload), orbitals, fitted))
            got = grid_exchange(sent).reshape(ngroups, nslots + 1, block_width)
            psi = jnp.concatenate(band_swap(rows_own), 1)
            fitted_got = jnp.stack(band_swap(fitted_own), 0)
            fitted_all = jnp.take(fitted_got, jnp.arange(nbands, dtype=jnp.int32) ^ band, axis=0)
            fitted_all = fitted_all.reshape(ngroups // 2, 2, nslots, fitted.shape[1])
            coll = jnp.concatenate(band_swap(pair_up(got[:, :nslots])), 1)
            first_filled = got[:, nslots, :nslots].reshape(ngroups // 2, 2, nslots)[:, 0] > 0
            fitted_all = jnp.where(
                first_filled[:, :, None], fitted_all[:, 0], jnp.flip(fitted_all[:, 1], axis=1)
            ).reshape(-1, fitted.shape[1]).astype(jnp.float32)
            orbital_block = psi.astype(jnp.bfloat16)
        else:
            own = psi[:, :block_width]
            at_slots = jnp.where(valid_mask[:, None], own[safe_idx], 0.0)
            nslots = at_slots.shape[0]
            payload = jnp.concatenate([at_slots, sq.reshape(nbands, block_width)], 0)
            got = grid_gather(payload).reshape(ngroups, nslots + nbands, block_width)
            total = jnp.sum(got[:, nslots:], axis=0).reshape(total_orbitals)
            scale = lax.rsqrt(total / (rows * ngroups) + 1e-06)
            coll_own = pair_up((got[:, :nslots] * scale[:block_width]).astype(jnp.bfloat16))
            coll = jnp.concatenate(band_swap(coll_own), 1)
            psi = psi * scale
            orbital_block = psi.astype(jnp.bfloat16)
        proj = None
        for k in range(nbands):
            part = lax.dot_general(
                coll[:, k * block_width:(k + 1) * block_width],
                orbital_block[:, k * block_width:(k + 1) * block_width],
                (((1,), (1,)), ((), ())),
                preferred_element_type=jnp.float32,
            )
            part = (part / total_orbitals).astype(jnp.bfloat16).astype(jnp.float32)
            proj = part if proj is None else proj + part
        tile_blocks = (fitted_all * proj).astype(jnp.bfloat16)
        applied = lax.dot_general(
            tile_blocks, coll, (((0,), (0,)), ((), ())), preferred_element_type=jnp.float32
        )
        psi = psi - 0.25 * (pot * psi - applied)
        sq = jnp.sum(psi * psi, axis=0)
    total = jnp.sum(grid_gather(sq[None, :block_width]), axis=0)
    return psi[:, :block_width] * lax.rsqrt(total / (rows * ngroups) + 1e-06)


def body_spread(orbitals, potential, fitted, points):
    rows = orbitals.shape[0]
    block_width = orbitals.shape[1]
    nbands = lax.axis_size("band")
    ngroups = lax.axis_size("grid")
    total_orbitals = block_width * nbands
    valid_mask = points >= 0
    safe_idx = jnp.where(valid_mask, points, 0)
    psi = orbitals
    for step in range(ITERS):
        orbital_block = psi.astype(jnp.bfloat16)
        selected_points = jnp.where(
            valid_mask[:, None], orbital_block[safe_idx], jnp.zeros((), jnp.bfloat16)
        )
        collocation_matrix = lax.all_gather(selected_points, "grid", axis=0, tiled=True)
        product = lax.dot_general(
            collocation_matrix,
            orbital_block,
            (((1,), (1,)), ((), ())),
            preferred_element_type=jnp.float32,
        )
        proj = lax.psum_scatter(
            (product / total_orbitals).astype(jnp.bfloat16), "band", scatter_dimension=0, tiled=True
        ).astype(jnp.float32)
        tile_blocks = (fitted.astype(jnp.float32) * proj).astype(jnp.bfloat16)
        orbitals_at_slots = lax.all_to_all(
            collocation_matrix, "band", split_axis=0, concat_axis=1, tiled=True
        )
        partial_value = lax.dot_general(
            tile_blocks,
            orbitals_at_slots,
            (((0,), (0,)), ((), ())),
            preferred_element_type=jnp.float32,
        )
        applied = lax.psum_scatter(
            partial_value.astype(jnp.bfloat16), "band", scatter_dimension=1, tiled=True
        ).astype(jnp.float32)
        fresh = psi - 0.25 * (potential[:, None] * psi - applied)
        squares = lax.psum(jnp.sum(fresh * fresh, axis=0), "grid")
        psi = fresh * lax.rsqrt(squares / (rows * ngroups) + 1e-06)
    return psi


def solution(mesh):
    in_specs = (P("grid", "band"), P("grid"), P("band", "grid"), P("grid"))
    out_specs = P("grid", "band")
    return jax.shard_map(body, mesh=mesh, in_specs=in_specs, out_specs=out_specs, check_vma=False)
```

```python
import jax
import jax.numpy as jnp
from jax import lax
from jax.sharding import PartitionSpec as P

ITERS = 2


def grid_copies(x):
    ngroups = lax.axis_size("grid")
    return jnp.broadcast_to(x[None], (ngroups,) + x.shape)


def grid_exchange(sent):
    got = lax.all_to_all(sent, "grid", 0, 0, tiled=True)
    return got.reshape((sent.shape[0] * sent.shape[1],) + sent.shape[2:])


def grid_gather(x):
    return grid_exchange(grid_copies(x))


def band_swap(x):
    nbands = lax.axis_size("band")
    got = [x]
    for k in range(1, nbands):
        got.append(lax.ppermute(x, "band", [(i, i ^ k) for i in range(nbands)]))
    return got


def pair_up(slots):
    ngroups, nslots = slots.shape[:2]
    pairs = slots.reshape((ngroups // 2, 2) + slots.shape[1:])
    return (pairs[:, 0] + jnp.flip(pairs[:, 1], axis=1)).reshape((ngroups // 2 * nslots,) + slots.shape[2:])


def tree_gather(slots, extra, merge_first, merge_extra):
    ngroups = lax.axis_size("grid")
    g = lax.axis_index("grid")
    nslots = slots.shape[0]
    got = lax.ppermute(jnp.concatenate([slots, extra], 0), "grid", [(i, i ^ 1) for i in range(ngroups)])
    lower = (g & 1) == 1
    first = jnp.where(lower, got[:nslots], slots)
    second = jnp.where(lower, slots, got[:nslots])
    cur = first + jnp.flip(second, axis=0)
    extra = merge_first(extra, got[nslots:], lower)
    step = 2
    while step < ngroups:
        got = lax.ppermute(jnp.concatenate([cur, extra], 0), "grid", [(i, i ^ step) for i in range(ngroups)])
        lower = (g & step) != 0
        n = cur.shape[0]
        cur = jnp.where(lower, jnp.concatenate([got[:n], cur], 0), jnp.concatenate([cur, got[:n]], 0))
        extra = merge_extra(extra, got[n:], lower)
        step *= 2
    return cur, extra


def add_extra(own, got, lower):
    return own + got


def body(orbitals, potential, fitted, points):
    if lax.axis_size("grid") > 8 or lax.axis_size("grid") & (lax.axis_size("grid") - 1) or points.shape[0] > orbitals.shape[1]:
        return body_spread(orbitals, potential, fitted, points)
    rows = orbitals.shape[0]
    block_width = orbitals.shape[1]
    nbands = lax.axis_size("band")
    ngroups = lax.axis_size("grid")
    band = lax.axis_index("band")
    total_orbitals = block_width * nbands
    valid_mask = points >= 0
    safe_idx = jnp.where(valid_mask, points, 0)
    pot = potential[:, None]
    sq = None
    for step in range(ITERS):
        if sq is None:
            nslots = points.shape[0]
            selected = jnp.where(valid_mask[:, None], orbitals[safe_idx], 0.0).astype(jnp.bfloat16)
            filled = jnp.pad(valid_mask.astype(jnp.bfloat16), (0, block_width - nslots))
            def pick_first(own, got, lower):
                return jnp.where(lower, got, own)

            def in_order(own, got, lower):
                return jnp.where(lower, jnp.concatenate([got, own], 0), jnp.concatenate([own, got], 0))

            sel, mask_row, rows_own, fitted_own = lax.optimization_barrier((selected, filled[None], orbitals, fitted))
            merged, first_rows = tree_gather(sel, mask_row, pick_first, in_order)
            psi = jnp.concatenate(band_swap(rows_own), 1)
            fitted_got = jnp.stack(band_swap(fitted_own), 0)
            fitted_all = jnp.take(fitted_got, jnp.arange(nbands, dtype=jnp.int32) ^ band, axis=0)
            fitted_all = fitted_all.reshape(ngroups // 2, 2, nslots, fitted.shape[1])
            coll = jnp.concatenate(band_swap(merged), 1)
            first_filled = first_rows[:, :nslots] > 0
            fitted_all = jnp.where(
                first_filled[:, :, None], fitted_all[:, 0], jnp.flip(fitted_all[:, 1], axis=1)
            ).reshape(-1, fitted.shape[1]).astype(jnp.float32)
            orbital_block = psi.astype(jnp.bfloat16)
        else:
            own = psi[:, :block_width]
            at_slots = jnp.where(valid_mask[:, None], own[safe_idx], 0.0)
            nslots = at_slots.shape[0]
            merged, total = tree_gather(at_slots, sq.reshape(nbands, block_width), add_extra, add_extra)
            scale = lax.rsqrt(total.reshape(total_orbitals) / (rows * ngroups) + 1e-06)
            coll_own = (merged * scale[:block_width]).astype(jnp.bfloat16)
            coll = jnp.concatenate(band_swap(coll_own), 1)
            psi = psi * scale
            orbital_block = psi.astype(jnp.bfloat16)
        proj = None
        for k in range(nbands):
            part = lax.dot_general(
                coll[:, k * block_width:(k + 1) * block_width],
                orbital_block[:, k * block_width:(k + 1) * block_width],
                (((1,), (1,)), ((), ())),
                preferred_element_type=jnp.float32,
            )
            part = (part / total_orbitals).astype(jnp.bfloat16).astype(jnp.float32)
            proj = part if proj is None else proj + part
        tile_blocks = (fitted_all * proj).astype(jnp.bfloat16)
        applied = lax.dot_general(
            tile_blocks, coll, (((0,), (0,)), ((), ())), preferred_element_type=jnp.float32
        )
        psi = psi - 0.25 * (pot * psi - applied)
        sq = jnp.sum(psi * psi, axis=0)
    total = sq[None, :block_width]
    step = 1
    while step < ngroups:
        total = total + lax.ppermute(total, "grid", [(i, i ^ step) for i in range(ngroups)])
        step *= 2
    return psi[:, :block_width] * lax.rsqrt(total / (rows * ngroups) + 1e-06)


def body_spread(orbitals, potential, fitted, points):
    rows = orbitals.shape[0]
    block_width = orbitals.shape[1]
    nbands = lax.axis_size("band")
    ngroups = lax.axis_size("grid")
    total_orbitals = block_width * nbands
    valid_mask = points >= 0
    safe_idx = jnp.where(valid_mask, points, 0)
    psi = orbitals
    for step in range(ITERS):
        orbital_block = psi.astype(jnp.bfloat16)
        selected_points = jnp.where(
            valid_mask[:, None], orbital_block[safe_idx], jnp.zeros((), jnp.bfloat16)
        )
        collocation_matrix = lax.all_gather(selected_points, "grid", axis=0, tiled=True)
        product = lax.dot_general(
            collocation_matrix,
            orbital_block,
            (((1,), (1,)), ((), ())),
            preferred_element_type=jnp.float32,
        )
        proj = lax.psum_scatter(
            (product / total_orbitals).astype(jnp.bfloat16), "band", scatter_dimension=0, tiled=True
        ).astype(jnp.float32)
        tile_blocks = (fitted.astype(jnp.float32) * proj).astype(jnp.bfloat16)
        orbitals_at_slots = lax.all_to_all(
            collocation_matrix, "band", split_axis=0, concat_axis=1, tiled=True
        )
        partial_value = lax.dot_general(
            tile_blocks,
            orbitals_at_slots,
            (((0,), (0,)), ((), ())),
            preferred_element_type=jnp.float32,
        )
        applied = lax.psum_scatter(
            partial_value.astype(jnp.bfloat16), "band", scatter_dimension=1, tiled=True
        ).astype(jnp.float32)
        fresh = psi - 0.25 * (potential[:, None] * psi - applied)
        squares = lax.psum(jnp.sum(fresh * fresh, axis=0), "grid")
        psi = fresh * lax.rsqrt(squares / (rows * ngroups) + 1e-06)
    return psi


def solution(mesh):
    in_specs = (P("grid", "band"), P("grid"), P("band", "grid"), P("grid"))
    out_specs = P("grid", "band")
    return jax.shard_map(body, mesh=mesh, in_specs=in_specs, out_specs=out_specs, check_vma=False)
```

```python
import jax
import jax.numpy as jnp
from jax import lax
from jax.sharding import PartitionSpec as P

ITERS = 2


def grid_copies(x):
    ngroups = lax.axis_size("grid")
    return jnp.broadcast_to(x[None], (ngroups,) + x.shape)


def grid_exchange(sent):
    got = lax.all_to_all(sent, "grid", 0, 0, tiled=True)
    return got.reshape((sent.shape[0] * sent.shape[1],) + sent.shape[2:])


def grid_gather(x):
    return grid_exchange(grid_copies(x))


def band_swap(x):
    nbands = lax.axis_size("band")
    got = [x]
    for k in range(1, nbands):
        got.append(lax.ppermute(x, "band", [(i, i ^ k) for i in range(nbands)]))
    return got


def pair_up(slots):
    ngroups, nslots = slots.shape[:2]
    pairs = slots.reshape((ngroups // 2, 2) + slots.shape[1:])
    return (pairs[:, 0] + jnp.flip(pairs[:, 1], axis=1)).reshape((ngroups // 2 * nslots,) + slots.shape[2:])


def tree_gather(slots, extra, merge_first, merge_extra):
    ngroups = lax.axis_size("grid")
    g = lax.axis_index("grid")
    nslots = slots.shape[0]
    got = lax.ppermute(jnp.concatenate([slots, extra], 0), "grid", [(i, i ^ 1) for i in range(ngroups)])
    lower = (g & 1) == 1
    first = jnp.where(lower, got[:nslots], slots)
    second = jnp.where(lower, slots, got[:nslots])
    cur = first + jnp.flip(second, axis=0)
    extra = merge_first(extra, got[nslots:], lower)
    step = 2
    while step < ngroups:
        got = lax.ppermute(jnp.concatenate([cur, extra], 0), "grid", [(i, i ^ step) for i in range(ngroups)])
        lower = (g & step) != 0
        n = cur.shape[0]
        cur = jnp.where(lower, jnp.concatenate([got[:n], cur], 0), jnp.concatenate([cur, got[:n]], 0))
        extra = merge_extra(extra, got[n:], lower)
        step *= 2
    return cur, extra


def body(orbitals, potential, fitted, points):
    if lax.axis_size("grid") > 8 or lax.axis_size("grid") & (lax.axis_size("grid") - 1) or points.shape[0] > orbitals.shape[1]:
        return body_spread(orbitals, potential, fitted, points)
    rows = orbitals.shape[0]
    block_width = orbitals.shape[1]
    nbands = lax.axis_size("band")
    ngroups = lax.axis_size("grid")
    band = lax.axis_index("band")
    total_orbitals = block_width * nbands
    valid_mask = points >= 0
    safe_idx = jnp.where(valid_mask, points, 0)
    pot = potential[:, None]
    sq = None
    for step in range(ITERS):
        if sq is None:
            nslots = points.shape[0]
            selected = jnp.where(valid_mask[:, None], orbitals[safe_idx], 0.0).astype(jnp.bfloat16)
            filled = jnp.pad(valid_mask.astype(jnp.bfloat16), (0, block_width - nslots))
            def pick_first(own, got, lower):
                return jnp.where(lower, got, own)

            def in_order(own, got, lower):
                return jnp.where(lower, jnp.concatenate([got, own], 0), jnp.concatenate([own, got], 0))

            sel, mask_row, rows_own, fitted_own = lax.optimization_barrier((selected, filled[None], orbitals, fitted))
            merged, first_rows = tree_gather(sel, mask_row, pick_first, in_order)
            psi = jnp.concatenate(band_swap(rows_own), 1)
            fitted_got = jnp.stack(band_swap(fitted_own), 0)
            fitted_all = jnp.take(fitted_got, jnp.arange(nbands, dtype=jnp.int32) ^ band, axis=0)
            fitted_all = fitted_all.reshape(ngroups // 2, 2, nslots, fitted.shape[1])
            coll = jnp.concatenate(band_swap(merged), 1)
            first_filled = first_rows[:, :nslots] > 0
            fitted_all = jnp.where(
                first_filled[:, :, None], fitted_all[:, 0], jnp.flip(fitted_all[:, 1], axis=1)
            ).reshape(-1, fitted.shape[1]).astype(jnp.float32)
            orbital_block = psi.astype(jnp.bfloat16)
        else:
            own = psi[:, :block_width]
            at_slots = jnp.where(valid_mask[:, None], own[safe_idx], 0.0)
            nslots = at_slots.shape[0]
            payload = jnp.concatenate([at_slots, sq.reshape(nbands, block_width)], 0)
            got = grid_gather(payload).reshape(ngroups, nslots + nbands, block_width)
            total = jnp.sum(got[:, nslots:], axis=0).reshape(total_orbitals)
            scale = lax.rsqrt(total / (rows * ngroups) + 1e-06)
            coll_own = pair_up((got[:, :nslots] * scale[:block_width]).astype(jnp.bfloat16))
            coll = jnp.concatenate(band_swap(coll_own), 1)
            psi = psi * scale
            orbital_block = psi.astype(jnp.bfloat16)
        proj = None
        for k in range(nbands):
            part = lax.dot_general(
                coll[:, k * block_width:(k + 1) * block_width],
                orbital_block[:, k * block_width:(k + 1) * block_width],
                (((1,), (1,)), ((), ())),
                preferred_element_type=jnp.float32,
            )
            part = (part / total_orbitals).astype(jnp.bfloat16).astype(jnp.float32)
            proj = part if proj is None else proj + part
        tile_blocks = (fitted_all * proj).astype(jnp.bfloat16)
        applied = lax.dot_general(
            tile_blocks, coll, (((0,), (0,)), ((), ())), preferred_element_type=jnp.float32
        )
        psi = psi - 0.25 * (pot * psi - applied)
        sq = jnp.sum(psi * psi, axis=0)
    total = jnp.sum(grid_gather(sq[None, :block_width]), axis=0)
    return psi[:, :block_width] * lax.rsqrt(total / (rows * ngroups) + 1e-06)


def body_spread(orbitals, potential, fitted, points):
    rows = orbitals.shape[0]
    block_width = orbitals.shape[1]
    nbands = lax.axis_size("band")
    ngroups = lax.axis_size("grid")
    total_orbitals = block_width * nbands
    valid_mask = points >= 0
    safe_idx = jnp.where(valid_mask, points, 0)
    psi = orbitals
    for step in range(ITERS):
        orbital_block = psi.astype(jnp.bfloat16)
        selected_points = jnp.where(
            valid_mask[:, None], orbital_block[safe_idx], jnp.zeros((), jnp.bfloat16)
        )
        collocation_matrix = lax.all_gather(selected_points, "grid", axis=0, tiled=True)
        product = lax.dot_general(
            collocation_matrix,
            orbital_block,
            (((1,), (1,)), ((), ())),
            preferred_element_type=jnp.float32,
        )
        proj = lax.psum_scatter(
            (product / total_orbitals).astype(jnp.bfloat16), "band", scatter_dimension=0, tiled=True
        ).astype(jnp.float32)
        tile_blocks = (fitted.astype(jnp.float32) * proj).astype(jnp.bfloat16)
        orbitals_at_slots = lax.all_to_all(
            collocation_matrix, "band", split_axis=0, concat_axis=1, tiled=True
        )
        partial_value = lax.dot_general(
            tile_blocks,
            orbitals_at_slots,
            (((0,), (0,)), ((), ())),
            preferred_element_type=jnp.float32,
        )
        applied = lax.psum_scatter(
            partial_value.astype(jnp.bfloat16), "band", scatter_dimension=1, tiled=True
        ).astype(jnp.float32)
        fresh = psi - 0.25 * (potential[:, None] * psi - applied)
        squares = lax.psum(jnp.sum(fresh * fresh, axis=0), "grid")
        psi = fresh * lax.rsqrt(squares / (rows * ngroups) + 1e-06)
    return psi


def solution(mesh):
    in_specs = (P("grid", "band"), P("grid"), P("band", "grid"), P("grid"))
    out_specs = P("grid", "band")
    return jax.shard_map(body, mesh=mesh, in_specs=in_specs, out_specs=out_specs, check_vma=False)
```

```python
import jax
import jax.numpy as jnp
from jax import lax
from jax.sharding import PartitionSpec as P

ITERS = 2


def grid_copies(x):
    ngroups = lax.axis_size("grid")
    return jnp.broadcast_to(x[None], (ngroups,) + x.shape)


def grid_exchange(sent):
    got = lax.all_to_all(sent, "grid", 0, 0, tiled=True)
    return got.reshape((sent.shape[0] * sent.shape[1],) + sent.shape[2:])


def grid_gather(x):
    return grid_exchange(grid_copies(x))


def band_swap(x):
    nbands = lax.axis_size("band")
    got = [x]
    for k in range(1, nbands):
        got.append(lax.ppermute(x, "band", [(i, i ^ k) for i in range(nbands)]))
    return got


def pair_up(slots):
    ngroups, nslots = slots.shape[:2]
    pairs = slots.reshape((ngroups // 2, 2) + slots.shape[1:])
    return (pairs[:, 0] + jnp.flip(pairs[:, 1], axis=1)).reshape((ngroups // 2 * nslots,) + slots.shape[2:])


def body(orbitals, potential, fitted, points):
    ngroups = lax.axis_size("grid")
    nbands = lax.axis_size("band")
    nslots = points.shape[0]
    block_width = orbitals.shape[1]
    if ngroups > 8 or ngroups % 2 or nbands & (nbands - 1) or nslots > block_width:
        return body_spread(orbitals, potential, fitted, points)
    rows = orbitals.shape[0]
    band = lax.axis_index("band")
    total_orbitals = block_width * nbands
    valid_mask = points >= 0
    safe_idx = jnp.where(valid_mask, points, 0)
    selected = jnp.where(valid_mask[:, None], orbitals[safe_idx], 0.0).astype(jnp.bfloat16)
    filled = jnp.pad(valid_mask.astype(jnp.bfloat16), (0, block_width - nslots))
    to_band = jnp.concatenate([orbitals.astype(jnp.bfloat16), fitted.reshape(-1, block_width)], 0)
    sent, to_band = lax.optimization_barrier((grid_copies(jnp.concatenate([selected, filled[None]], 0)), to_band))
    got = grid_exchange(sent).reshape(ngroups, nslots + 1, block_width)
    swapped = band_swap(to_band)
    rows_b = jnp.concatenate([part[:rows] for part in swapped], 1)
    fitted_got = jnp.stack([part[rows:].reshape(fitted.shape) for part in swapped], 0)
    fitted_all = jnp.take(fitted_got, jnp.arange(nbands, dtype=jnp.int32) ^ band, axis=0)
    fitted_all = fitted_all.reshape(ngroups // 2, 2, nslots, fitted.shape[1])
    coll = jnp.concatenate(band_swap(pair_up(got[:, :nslots])), 1)
    first_filled = got[:, nslots, :nslots].reshape(ngroups // 2, 2, nslots)[:, 0] > 0
    fitted_all = jnp.where(
        first_filled[:, :, None], fitted_all[:, 0], jnp.flip(fitted_all[:, 1], axis=1)
    ).reshape(-1, fitted.shape[1]).astype(jnp.float32)
    psi = orbitals
    pot = potential[:, None]
    for step in range(ITERS):
        if step:
            at_slots = jnp.where(valid_mask[:, None], psi[safe_idx], 0.0)
            got = grid_gather(jnp.concatenate([at_slots, sq[None]], 0)).reshape(ngroups, nslots + 1, block_width)
            total = jnp.sum(got[:, nslots], axis=0)
            scale = lax.rsqrt(total / (rows * ngroups) + 1e-06)
            coll_own = pair_up((got[:, :nslots] * scale).astype(jnp.bfloat16))
            psi = psi * scale
            ncoll = coll_own.shape[0]
            swapped = band_swap(jnp.concatenate([coll_own, psi.astype(jnp.bfloat16)], 0))
            coll = jnp.concatenate([part[:ncoll] for part in swapped], 1)
            rows_b = jnp.concatenate([part[ncoll:] for part in swapped], 1)
        proj = None
        for k in range(nbands):
            part = lax.dot_general(
                coll[:, k * block_width:(k + 1) * block_width],
                rows_b[:, k * block_width:(k + 1) * block_width],
                (((1,), (1,)), ((), ())),
                preferred_element_type=jnp.float32,
            )
            part = (part / total_orbitals).astype(jnp.bfloat16).astype(jnp.float32)
            proj = part if proj is None else proj + part
        tile_blocks = (fitted_all * proj).astype(jnp.bfloat16)
        applied = lax.dot_general(
            tile_blocks, coll[:, :block_width], (((0,), (0,)), ((), ())), preferred_element_type=jnp.float32
        )
        psi = psi - 0.25 * (pot * psi - applied)
        sq = jnp.sum(psi * psi, axis=0)
    total = jnp.sum(grid_gather(sq[None]), axis=0)
    return psi * lax.rsqrt(total / (rows * ngroups) + 1e-06)


def body_spread(orbitals, potential, fitted, points):
    rows = orbitals.shape[0]
    block_width = orbitals.shape[1]
    nbands = lax.axis_size("band")
    ngroups = lax.axis_size("grid")
    total_orbitals = block_width * nbands
    valid_mask = points >= 0
    safe_idx = jnp.where(valid_mask, points, 0)
    psi = orbitals
    for step in range(ITERS):
        orbital_block = psi.astype(jnp.bfloat16)
        selected_points = jnp.where(
            valid_mask[:, None], orbital_block[safe_idx], jnp.zeros((), jnp.bfloat16)
        )
        collocation_matrix = lax.all_gather(selected_points, "grid", axis=0, tiled=True)
        product = lax.dot_general(
            collocation_matrix,
            orbital_block,
            (((1,), (1,)), ((), ())),
            preferred_element_type=jnp.float32,
        )
        proj = lax.psum_scatter(
            (product / total_orbitals).astype(jnp.bfloat16), "band", scatter_dimension=0, tiled=True
        ).astype(jnp.float32)
        tile_blocks = (fitted.astype(jnp.float32) * proj).astype(jnp.bfloat16)
        orbitals_at_slots = lax.all_to_all(
            collocation_matrix, "band", split_axis=0, concat_axis=1, tiled=True
        )
        partial_value = lax.dot_general(
            tile_blocks,
            orbitals_at_slots,
            (((0,), (0,)), ((), ())),
            preferred_element_type=jnp.float32,
        )
        applied = lax.psum_scatter(
            partial_value.astype(jnp.bfloat16), "band", scatter_dimension=1, tiled=True
        ).astype(jnp.float32)
        fresh = psi - 0.25 * (potential[:, None] * psi - applied)
        squares = lax.psum(jnp.sum(fresh * fresh, axis=0), "grid")
        psi = fresh * lax.rsqrt(squares / (rows * ngroups) + 1e-06)
    return psi


def solution(mesh):
    in_specs = (P("grid", "band"), P("grid"), P("band", "grid"), P("grid"))
    out_specs = P("grid", "band")
    return jax.shard_map(body, mesh=mesh, in_specs=in_specs, out_specs=out_specs, check_vma=False)
```

```python
import jax
import jax.numpy as jnp
from jax import lax
from jax.sharding import PartitionSpec as P

ITERS = 2


def grid_copies(x):
    ngroups = lax.axis_size("grid")
    return jnp.broadcast_to(x[None], (ngroups,) + x.shape)


def grid_exchange(sent):
    got = lax.all_to_all(sent, "grid", 0, 0, tiled=True)
    return got.reshape((sent.shape[0] * sent.shape[1],) + sent.shape[2:])


def grid_gather(x):
    return grid_exchange(grid_copies(x))


def band_swap(x):
    nbands = lax.axis_size("band")
    got = [x]
    for k in range(1, nbands):
        got.append(lax.ppermute(x, "band", [(i, i ^ k) for i in range(nbands)]))
    return got


def pair_up(slots):
    ngroups, nslots = slots.shape[:2]
    pairs = slots.reshape((ngroups // 2, 2) + slots.shape[1:])
    return (pairs[:, 0] + jnp.flip(pairs[:, 1], axis=1)).reshape((ngroups // 2 * nslots,) + slots.shape[2:])


def body(orbitals, potential, fitted, points):
    ngroups = lax.axis_size("grid")
    nbands = lax.axis_size("band")
    nslots = points.shape[0]
    block_width = orbitals.shape[1]
    if ngroups > 8 or ngroups % 2 or nbands & (nbands - 1) or nslots > block_width:
        return body_spread(orbitals, potential, fitted, points)
    rows = orbitals.shape[0]
    band = lax.axis_index("band")
    total_orbitals = block_width * nbands
    valid_mask = points >= 0
    safe_idx = jnp.where(valid_mask, points, 0)
    selected = jnp.where(valid_mask[:, None], orbitals[safe_idx], 0.0).astype(jnp.bfloat16)
    filled = jnp.pad(valid_mask.astype(jnp.bfloat16), (0, block_width - nslots))
    to_band = jnp.concatenate([orbitals.astype(jnp.bfloat16), fitted.reshape(-1, block_width)], 0)
    sent, to_band = lax.optimization_barrier((grid_copies(jnp.concatenate([selected, filled[None]], 0)), to_band))
    got = grid_exchange(sent).reshape(ngroups, nslots + 1, block_width)
    swapped = band_swap(to_band)
    rows_b = jnp.concatenate([part[:rows] for part in swapped], 1)
    fitted_got = jnp.stack([part[rows:].reshape(fitted.shape) for part in swapped], 0)
    fitted_all = jnp.take(fitted_got, jnp.arange(nbands, dtype=jnp.int32) ^ band, axis=0)
    fitted_all = fitted_all.reshape(ngroups // 2, 2, nslots, fitted.shape[1])
    coll = jnp.concatenate(band_swap(pair_up(got[:, :nslots])), 1)
    first_filled = got[:, nslots, :nslots].reshape(ngroups // 2, 2, nslots)[:, 0] > 0
    fitted_all = jnp.where(
        first_filled[:, :, None], fitted_all[:, 0], jnp.flip(fitted_all[:, 1], axis=1)
    ).reshape(-1, fitted.shape[1]).astype(jnp.float32)
    psi = orbitals
    pot = potential[:, None]
    for step in range(ITERS):
        if step:
            at_slots = jnp.where(valid_mask[:, None], psi[safe_idx], 0.0).astype(jnp.bfloat16)
            high = lax.reduce_precision(sq, exponent_bits=8, mantissa_bits=7)
            rest = sq - high
            middle = lax.reduce_precision(rest, exponent_bits=8, mantissa_bits=7)
            low = lax.reduce_precision(rest - middle, exponent_bits=8, mantissa_bits=7)
            parts = jnp.stack([high, middle, low], 0).astype(jnp.bfloat16)
            got = grid_gather(jnp.concatenate([at_slots, parts], 0)).reshape(ngroups, nslots + 3, block_width)
            sums = got[:, nslots:].astype(jnp.float32)
            total = jnp.sum((sums[:, 0] + sums[:, 1]) + sums[:, 2], axis=0)
            scale = lax.rsqrt(total / (rows * ngroups) + 1e-06)
            coll_own = pair_up((got[:, :nslots].astype(jnp.float32) * scale).astype(jnp.bfloat16))
            psi = psi * scale
            ncoll = coll_own.shape[0]
            swapped = band_swap(jnp.concatenate([coll_own, psi.astype(jnp.bfloat16)], 0))
            coll = jnp.concatenate([part[:ncoll] for part in swapped], 1)
            rows_b = jnp.concatenate([part[ncoll:] for part in swapped], 1)
        proj = None
        for k in range(nbands):
            part = lax.dot_general(
                coll[:, k * block_width:(k + 1) * block_width],
                rows_b[:, k * block_width:(k + 1) * block_width],
                (((1,), (1,)), ((), ())),
                preferred_element_type=jnp.float32,
            )
            part = (part / total_orbitals).astype(jnp.bfloat16).astype(jnp.float32)
            proj = part if proj is None else proj + part
        tile_blocks = (fitted_all * proj).astype(jnp.bfloat16)
        applied = lax.dot_general(
            tile_blocks, coll[:, :block_width], (((0,), (0,)), ((), ())), preferred_element_type=jnp.float32
        )
        psi = psi - 0.25 * (pot * psi - applied)
        sq = jnp.sum(psi * psi, axis=0)
    total = jnp.sum(grid_gather(sq[None]), axis=0)
    return psi * lax.rsqrt(total / (rows * ngroups) + 1e-06)


def body_spread(orbitals, potential, fitted, points):
    rows = orbitals.shape[0]
    block_width = orbitals.shape[1]
    nbands = lax.axis_size("band")
    ngroups = lax.axis_size("grid")
    total_orbitals = block_width * nbands
    valid_mask = points >= 0
    safe_idx = jnp.where(valid_mask, points, 0)
    psi = orbitals
    for step in range(ITERS):
        orbital_block = psi.astype(jnp.bfloat16)
        selected_points = jnp.where(
            valid_mask[:, None], orbital_block[safe_idx], jnp.zeros((), jnp.bfloat16)
        )
        collocation_matrix = lax.all_gather(selected_points, "grid", axis=0, tiled=True)
        product = lax.dot_general(
            collocation_matrix,
            orbital_block,
            (((1,), (1,)), ((), ())),
            preferred_element_type=jnp.float32,
        )
        proj = lax.psum_scatter(
            (product / total_orbitals).astype(jnp.bfloat16), "band", scatter_dimension=0, tiled=True
        ).astype(jnp.float32)
        tile_blocks = (fitted.astype(jnp.float32) * proj).astype(jnp.bfloat16)
        orbitals_at_slots = lax.all_to_all(
            collocation_matrix, "band", split_axis=0, concat_axis=1, tiled=True
        )
        partial_value = lax.dot_general(
            tile_blocks,
            orbitals_at_slots,
            (((0,), (0,)), ((), ())),
            preferred_element_type=jnp.float32,
        )
        applied = lax.psum_scatter(
            partial_value.astype(jnp.bfloat16), "band", scatter_dimension=1, tiled=True
        ).astype(jnp.float32)
        fresh = psi - 0.25 * (potential[:, None] * psi - applied)
        squares = lax.psum(jnp.sum(fresh * fresh, axis=0), "grid")
        psi = fresh * lax.rsqrt(squares / (rows * ngroups) + 1e-06)
    return psi


def solution(mesh):
    in_specs = (P("grid", "band"), P("grid"), P("band", "grid"), P("grid"))
    out_specs = P("grid", "band")
    return jax.shard_map(body, mesh=mesh, in_specs=in_specs, out_specs=out_specs, check_vma=False)
```

```python
import jax
import jax.numpy as jnp
from jax import lax
from jax.sharding import PartitionSpec as P

ITERS = 2


def grid_copies(x):
    ngroups = lax.axis_size("grid")
    return jnp.broadcast_to(x[None], (ngroups,) + x.shape)


def grid_exchange(sent):
    got = lax.all_to_all(sent, "grid", 0, 0, tiled=True)
    return got.reshape((sent.shape[0] * sent.shape[1],) + sent.shape[2:])


def grid_gather(x):
    return grid_exchange(grid_copies(x))


def band_swap(x):
    nbands = lax.axis_size("band")
    got = [x]
    for k in range(1, nbands):
        got.append(lax.ppermute(x, "band", [(i, i ^ k) for i in range(nbands)]))
    return got


def pair_up(slots):
    ngroups, nslots = slots.shape[:2]
    pairs = slots.reshape((ngroups // 2, 2) + slots.shape[1:])
    return (pairs[:, 0] + jnp.flip(pairs[:, 1], axis=1)).reshape((ngroups // 2 * nslots,) + slots.shape[2:])


def band_hops(x):
    nbands = lax.axis_size("band")
    held = {0: x}
    bit = nbands // 2
    while bit:
        keys = sorted(held)
        got = lax.ppermute(jnp.concatenate([held[k] for k in keys], 0), "band", [(i, i ^ bit) for i in range(nbands)])
        for n, k in enumerate(keys):
            held[k ^ bit] = got[n * x.shape[0]:(n + 1) * x.shape[0]]
        bit //= 2
    return [held[k] for k in range(nbands)]


def body(orbitals, potential, fitted, points):
    ngroups = lax.axis_size("grid")
    nbands = lax.axis_size("band")
    nslots = points.shape[0]
    block_width = orbitals.shape[1]
    if ngroups > 8 or ngroups % 2 or nbands & (nbands - 1) or nslots > block_width:
        return body_spread(orbitals, potential, fitted, points)
    rows = orbitals.shape[0]
    band = lax.axis_index("band")
    total_orbitals = block_width * nbands
    valid_mask = points >= 0
    safe_idx = jnp.where(valid_mask, points, 0)
    selected = jnp.where(valid_mask[:, None], orbitals[safe_idx], 0.0).astype(jnp.bfloat16)
    filled = jnp.pad(valid_mask.astype(jnp.bfloat16), (0, block_width - nslots))
    to_band = jnp.concatenate([orbitals.astype(jnp.bfloat16), fitted.reshape(-1, block_width)], 0)
    sent, to_band = lax.optimization_barrier((grid_copies(jnp.concatenate([selected, filled[None]], 0)), to_band))
    got = grid_exchange(sent).reshape(ngroups, nslots + 1, block_width)
    swapped = band_swap(to_band)
    rows_b = jnp.concatenate([part[:rows] for part in swapped], 1)
    fitted_got = jnp.stack([part[rows:].reshape(fitted.shape) for part in swapped], 0)
    fitted_all = jnp.take(fitted_got, jnp.arange(nbands, dtype=jnp.int32) ^ band, axis=0)
    fitted_all = fitted_all.reshape(ngroups // 2, 2, nslots, fitted.shape[1])
    coll = jnp.concatenate(band_hops(pair_up(got[:, :nslots])), 1)
    first_filled = got[:, nslots, :nslots].reshape(ngroups // 2, 2, nslots)[:, 0] > 0
    fitted_all = jnp.where(
        first_filled[:, :, None], fitted_all[:, 0], jnp.flip(fitted_all[:, 1], axis=1)
    ).reshape(-1, fitted.shape[1]).astype(jnp.float32)
    psi = orbitals
    pot = potential[:, None]
    for step in range(ITERS):
        if step:
            at_slots = jnp.where(valid_mask[:, None], psi[safe_idx], 0.0).astype(jnp.bfloat16)
            high = lax.reduce_precision(sq, exponent_bits=8, mantissa_bits=7)
            rest = sq - high
            middle = lax.reduce_precision(rest, exponent_bits=8, mantissa_bits=7)
            low = lax.reduce_precision(rest - middle, exponent_bits=8, mantissa_bits=7)
            parts = jnp.stack([high, middle, low], 0).astype(jnp.bfloat16)
            got = grid_gather(jnp.concatenate([at_slots, parts], 0)).reshape(ngroups, nslots + 3, block_width)
            sums = got[:, nslots:].astype(jnp.float32)
            total = jnp.sum((sums[:, 0] + sums[:, 1]) + sums[:, 2], axis=0)
            scale = lax.rsqrt(total / (rows * ngroups) + 1e-06)
            coll_own = pair_up((got[:, :nslots].astype(jnp.float32) * scale).astype(jnp.bfloat16))
            psi = psi * scale
            ncoll = coll_own.shape[0]
            swapped = band_hops(jnp.concatenate([coll_own, psi.astype(jnp.bfloat16)], 0))
            coll = jnp.concatenate([part[:ncoll] for part in swapped], 1)
            rows_b = jnp.concatenate([part[ncoll:] for part in swapped], 1)
        proj = None
        for k in range(nbands):
            part = lax.dot_general(
                coll[:, k * block_width:(k + 1) * block_width],
                rows_b[:, k * block_width:(k + 1) * block_width],
                (((1,), (1,)), ((), ())),
                preferred_element_type=jnp.float32,
            )
            part = (part / total_orbitals).astype(jnp.bfloat16).astype(jnp.float32)
            proj = part if proj is None else proj + part
        tile_blocks = (fitted_all * proj).astype(jnp.bfloat16)
        applied = lax.dot_general(
            tile_blocks, coll[:, :block_width], (((0,), (0,)), ((), ())), preferred_element_type=jnp.float32
        )
        psi = psi - 0.25 * (pot * psi - applied)
        sq = jnp.sum(psi * psi, axis=0)
    total = jnp.sum(grid_gather(sq[None]), axis=0)
    return psi * lax.rsqrt(total / (rows * ngroups) + 1e-06)


def body_spread(orbitals, potential, fitted, points):
    rows = orbitals.shape[0]
    block_width = orbitals.shape[1]
    nbands = lax.axis_size("band")
    ngroups = lax.axis_size("grid")
    total_orbitals = block_width * nbands
    valid_mask = points >= 0
    safe_idx = jnp.where(valid_mask, points, 0)
    psi = orbitals
    for step in range(ITERS):
        orbital_block = psi.astype(jnp.bfloat16)
        selected_points = jnp.where(
            valid_mask[:, None], orbital_block[safe_idx], jnp.zeros((), jnp.bfloat16)
        )
        collocation_matrix = lax.all_gather(selected_points, "grid", axis=0, tiled=True)
        product = lax.dot_general(
            collocation_matrix,
            orbital_block,
            (((1,), (1,)), ((), ())),
            preferred_element_type=jnp.float32,
        )
        proj = lax.psum_scatter(
            (product / total_orbitals).astype(jnp.bfloat16), "band", scatter_dimension=0, tiled=True
        ).astype(jnp.float32)
        tile_blocks = (fitted.astype(jnp.float32) * proj).astype(jnp.bfloat16)
        orbitals_at_slots = lax.all_to_all(
            collocation_matrix, "band", split_axis=0, concat_axis=1, tiled=True
        )
        partial_value = lax.dot_general(
            tile_blocks,
            orbitals_at_slots,
            (((0,), (0,)), ((), ())),
            preferred_element_type=jnp.float32,
        )
        applied = lax.psum_scatter(
            partial_value.astype(jnp.bfloat16), "band", scatter_dimension=1, tiled=True
        ).astype(jnp.float32)
        fresh = psi - 0.25 * (potential[:, None] * psi - applied)
        squares = lax.psum(jnp.sum(fresh * fresh, axis=0), "grid")
        psi = fresh * lax.rsqrt(squares / (rows * ngroups) + 1e-06)
    return psi


def solution(mesh):
    in_specs = (P("grid", "band"), P("grid"), P("band", "grid"), P("grid"))
    out_specs = P("grid", "band")
    return jax.shard_map(body, mesh=mesh, in_specs=in_specs, out_specs=out_specs, check_vma=False)
```

```python
import jax
import jax.numpy as jnp
from jax import lax
from jax.sharding import PartitionSpec as P

ITERS = 2


def grid_copies(x):
    ngroups = lax.axis_size("grid")
    return jnp.broadcast_to(x[None], (ngroups,) + x.shape)


def grid_exchange(sent):
    got = lax.all_to_all(sent, "grid", 0, 0, tiled=True)
    return got.reshape((sent.shape[0] * sent.shape[1],) + sent.shape[2:])


def grid_gather(x):
    return grid_exchange(grid_copies(x))


def band_swap(x):
    nbands = lax.axis_size("band")
    got = [x]
    for k in range(1, nbands):
        got.append(lax.ppermute(x, "band", [(i, i ^ k) for i in range(nbands)]))
    return got


def pair_up(slots):
    ngroups, nslots = slots.shape[:2]
    pairs = slots.reshape((ngroups // 2, 2) + slots.shape[1:])
    return (pairs[:, 0] + jnp.flip(pairs[:, 1], axis=1)).reshape((ngroups // 2 * nslots,) + slots.shape[2:])


def band_hops(x):
    nbands = lax.axis_size("band")
    held = {0: x}
    bit = nbands // 2
    while bit:
        keys = sorted(held)
        got = lax.ppermute(jnp.concatenate([held[k] for k in keys], 0), "band", [(i, i ^ bit) for i in range(nbands)])
        for n, k in enumerate(keys):
            held[k ^ bit] = got[n * x.shape[0]:(n + 1) * x.shape[0]]
        bit //= 2
    return [held[k] for k in range(nbands)]


def body(orbitals, potential, fitted, points):
    ngroups = lax.axis_size("grid")
    nbands = lax.axis_size("band")
    nslots = points.shape[0]
    block_width = orbitals.shape[1]
    if ngroups > 8 or ngroups % 2 or nbands & (nbands - 1) or nslots > block_width:
        return body_spread(orbitals, potential, fitted, points)
    rows = orbitals.shape[0]
    band = lax.axis_index("band")
    total_orbitals = block_width * nbands
    valid_mask = points >= 0
    picks = (points[:, None] == jnp.arange(rows, dtype=points.dtype)[None, :]).astype(jnp.bfloat16)
    rows_b16 = orbitals.astype(jnp.bfloat16)
    selected = jnp.dot(picks, rows_b16, preferred_element_type=jnp.float32).astype(jnp.bfloat16)
    filled = jnp.pad(valid_mask.astype(jnp.bfloat16), (0, block_width - nslots))
    to_band = jnp.concatenate([rows_b16, fitted.reshape(-1, block_width)], 0)
    sent, to_band = lax.optimization_barrier((grid_copies(jnp.concatenate([selected, filled[None]], 0)), to_band))
    got = grid_exchange(sent).reshape(ngroups, nslots + 1, block_width)
    swapped = band_swap(to_band)
    rows_b = jnp.concatenate([part[:rows] for part in swapped], 1)
    fitted_got = jnp.stack([part[rows:].reshape(fitted.shape) for part in swapped], 0)
    fitted_all = jnp.take(fitted_got, jnp.arange(nbands, dtype=jnp.int32) ^ band, axis=0)
    fitted_all = fitted_all.reshape(ngroups // 2, 2, nslots, fitted.shape[1])
    coll = jnp.concatenate(band_hops(pair_up(got[:, :nslots])), 1)
    first_filled = got[:, nslots, :nslots].reshape(ngroups // 2, 2, nslots)[:, 0] > 0
    fitted_all = jnp.where(
        first_filled[:, :, None], fitted_all[:, 0], jnp.flip(fitted_all[:, 1], axis=1)
    ).reshape(-1, fitted.shape[1]).astype(jnp.float32)
    psi = orbitals
    pot = potential[:, None]
    for step in range(ITERS):
        if step:
            at_slots = jnp.dot(picks, psi, preferred_element_type=jnp.float32).astype(jnp.bfloat16)
            high = lax.reduce_precision(sq, exponent_bits=8, mantissa_bits=7)
            rest = sq - high
            middle = lax.reduce_precision(rest, exponent_bits=8, mantissa_bits=7)
            low = lax.reduce_precision(rest - middle, exponent_bits=8, mantissa_bits=7)
            parts = jnp.stack([high, middle, low], 0).astype(jnp.bfloat16)
            got = grid_gather(jnp.concatenate([at_slots, parts], 0)).reshape(ngroups, nslots + 3, block_width)
            sums = got[:, nslots:].astype(jnp.float32)
            total = jnp.sum((sums[:, 0] + sums[:, 1]) + sums[:, 2], axis=0)
            scale = lax.rsqrt(total / (rows * ngroups) + 1e-06)
            coll_own = pair_up((got[:, :nslots].astype(jnp.float32) * scale).astype(jnp.bfloat16))
            psi = psi * scale
            ncoll = coll_own.shape[0]
            swapped = band_hops(jnp.concatenate([coll_own, psi.astype(jnp.bfloat16)], 0))
            coll = jnp.concatenate([part[:ncoll] for part in swapped], 1)
            rows_b = jnp.concatenate([part[ncoll:] for part in swapped], 1)
        proj = None
        for k in range(nbands):
            part = lax.dot_general(
                coll[:, k * block_width:(k + 1) * block_width],
                rows_b[:, k * block_width:(k + 1) * block_width],
                (((1,), (1,)), ((), ())),
                preferred_element_type=jnp.float32,
            )
            part = (part / total_orbitals).astype(jnp.bfloat16).astype(jnp.float32)
            proj = part if proj is None else proj + part
        tile_blocks = (fitted_all * proj).astype(jnp.bfloat16)
        applied = lax.dot_general(
            tile_blocks, coll[:, :block_width], (((0,), (0,)), ((), ())), preferred_element_type=jnp.float32
        )
        psi = psi - 0.25 * (pot * psi - applied)
        sq = jnp.sum(psi * psi, axis=0)
    total = jnp.sum(grid_gather(sq[None]), axis=0)
    return psi * lax.rsqrt(total / (rows * ngroups) + 1e-06)


def body_spread(orbitals, potential, fitted, points):
    rows = orbitals.shape[0]
    block_width = orbitals.shape[1]
    nbands = lax.axis_size("band")
    ngroups = lax.axis_size("grid")
    total_orbitals = block_width * nbands
    valid_mask = points >= 0
    safe_idx = jnp.where(valid_mask, points, 0)
    psi = orbitals
    for step in range(ITERS):
        orbital_block = psi.astype(jnp.bfloat16)
        selected_points = jnp.where(
            valid_mask[:, None], orbital_block[safe_idx], jnp.zeros((), jnp.bfloat16)
        )
        collocation_matrix = lax.all_gather(selected_points, "grid", axis=0, tiled=True)
        product = lax.dot_general(
            collocation_matrix,
            orbital_block,
            (((1,), (1,)), ((), ())),
            preferred_element_type=jnp.float32,
        )
        proj = lax.psum_scatter(
            (product / total_orbitals).astype(jnp.bfloat16), "band", scatter_dimension=0, tiled=True
        ).astype(jnp.float32)
        tile_blocks = (fitted.astype(jnp.float32) * proj).astype(jnp.bfloat16)
        orbitals_at_slots = lax.all_to_all(
            collocation_matrix, "band", split_axis=0, concat_axis=1, tiled=True
        )
        partial_value = lax.dot_general(
            tile_blocks,
            orbitals_at_slots,
            (((0,), (0,)), ((), ())),
            preferred_element_type=jnp.float32,
        )
        applied = lax.psum_scatter(
            partial_value.astype(jnp.bfloat16), "band", scatter_dimension=1, tiled=True
        ).astype(jnp.float32)
        fresh = psi - 0.25 * (potential[:, None] * psi - applied)
        squares = lax.psum(jnp.sum(fresh * fresh, axis=0), "grid")
        psi = fresh * lax.rsqrt(squares / (rows * ngroups) + 1e-06)
    return psi


def solution(mesh):
    in_specs = (P("grid", "band"), P("grid"), P("band", "grid"), P("grid"))
    out_specs = P("grid", "band")
    return jax.shard_map(body, mesh=mesh, in_specs=in_specs, out_specs=out_specs, check_vma=False)
```

```python
import jax
import jax.numpy as jnp
from jax import lax
from jax.sharding import PartitionSpec as P

ITERS = 2


def grid_copies(x):
    ngroups = lax.axis_size("grid")
    return jnp.broadcast_to(x[None], (ngroups,) + x.shape)


def grid_exchange(sent):
    got = lax.all_to_all(sent, "grid", 0, 0, tiled=True)
    return got.reshape((sent.shape[0] * sent.shape[1],) + sent.shape[2:])


def grid_gather(x):
    return grid_exchange(grid_copies(x))


def band_swap(x):
    nbands = lax.axis_size("band")
    got = [x]
    for k in range(1, nbands):
        got.append(lax.ppermute(x, "band", [(i, i ^ k) for i in range(nbands)]))
    return got


def pair_up(slots):
    ngroups, nslots = slots.shape[:2]
    pairs = slots.reshape((ngroups // 2, 2) + slots.shape[1:])
    return (pairs[:, 0] + jnp.flip(pairs[:, 1], axis=1)).reshape((ngroups // 2 * nslots,) + slots.shape[2:])


def band_hops(x):
    nbands = lax.axis_size("band")
    held = {0: x}
    bit = nbands // 2
    while bit:
        keys = sorted(held)
        got = lax.ppermute(jnp.concatenate([held[k] for k in keys], 0), "band", [(i, i ^ bit) for i in range(nbands)])
        for n, k in enumerate(keys):
            held[k ^ bit] = got[n * x.shape[0]:(n + 1) * x.shape[0]]
        bit //= 2
    return [held[k] for k in range(nbands)]


def body(orbitals, potential, fitted, points):
    ngroups = lax.axis_size("grid")
    nbands = lax.axis_size("band")
    nslots = points.shape[0]
    block_width = orbitals.shape[1]
    if ngroups > 8 or ngroups % 2 or nbands & (nbands - 1) or nslots > block_width:
        return body_spread(orbitals, potential, fitted, points)
    rows = orbitals.shape[0]
    band = lax.axis_index("band")
    total_orbitals = block_width * nbands
    valid_mask = points >= 0
    picks = (points[:, None] == jnp.arange(rows, dtype=points.dtype)[None, :]).astype(jnp.bfloat16)
    selected = jnp.dot(picks, orbitals.astype(jnp.bfloat16), preferred_element_type=jnp.float32).astype(jnp.bfloat16)
    filled = jnp.pad(valid_mask.astype(jnp.bfloat16), (0, block_width - nslots))
    to_band = jnp.concatenate([orbitals, fitted.reshape(-1, block_width).astype(jnp.float32)], 0)
    sent, to_band = lax.optimization_barrier((grid_copies(jnp.concatenate([selected, filled[None]], 0)), to_band))
    got = grid_exchange(sent).reshape(ngroups, nslots + 1, block_width)
    swapped = band_swap(to_band)
    psi = jnp.concatenate([part[:rows] for part in swapped], 1)
    fitted_got = jnp.stack([part[rows:].reshape(fitted.shape) for part in swapped], 0)
    fitted_all = jnp.take(fitted_got, jnp.arange(nbands, dtype=jnp.int32) ^ band, axis=0)
    fitted_all = fitted_all.reshape(ngroups // 2, 2, nslots, fitted.shape[1])
    coll = jnp.concatenate(band_hops(pair_up(got[:, :nslots])), 1)
    first_filled = got[:, nslots, :nslots].reshape(ngroups // 2, 2, nslots)[:, 0] > 0
    fitted_all = jnp.where(first_filled[:, :, None], fitted_all[:, 0], jnp.flip(fitted_all[:, 1], axis=1))
    fitted_all = fitted_all.reshape(-1, fitted.shape[1])
    pot = potential[:, None]
    for step in range(ITERS):
        last = step == ITERS - 1
        if step:
            at_slots = jnp.dot(picks, psi, preferred_element_type=jnp.float32).astype(jnp.bfloat16)
            high = lax.reduce_precision(sq, exponent_bits=8, mantissa_bits=7)
            rest = sq - high
            middle = lax.reduce_precision(rest, exponent_bits=8, mantissa_bits=7)
            low = lax.reduce_precision(rest - middle, exponent_bits=8, mantissa_bits=7)
            parts = jnp.stack([high, middle, low], 0).astype(jnp.bfloat16)
            got = grid_gather(jnp.concatenate([at_slots, parts], 0)).reshape(ngroups, nslots + 3, total_orbitals)
            sums = got[:, nslots:].astype(jnp.float32)
            total = jnp.sum((sums[:, 0] + sums[:, 1]) + sums[:, 2], axis=0)
            scale = lax.rsqrt(total / (rows * ngroups) + 1e-06)
            coll = pair_up((got[:, :nslots].astype(jnp.float32) * scale).astype(jnp.bfloat16))
            psi = psi * scale
        rows_b = psi.astype(jnp.bfloat16)
        proj = None
        for k in range(nbands):
            part = lax.dot_general(
                coll[:, k * block_width:(k + 1) * block_width],
                rows_b[:, k * block_width:(k + 1) * block_width],
                (((1,), (1,)), ((), ())),
                preferred_element_type=jnp.float32,
            )
            part = (part / total_orbitals).astype(jnp.bfloat16).astype(jnp.float32)
            proj = part if proj is None else proj + part
        tile_blocks = (fitted_all * proj).astype(jnp.bfloat16)
        if last:
            coll = coll[:, :block_width]
            psi = psi[:, :block_width]
        applied = lax.dot_general(
            tile_blocks, coll, (((0,), (0,)), ((), ())), preferred_element_type=jnp.float32
        )
        psi = psi - 0.25 * (pot * psi - applied)
        sq = jnp.sum(psi * psi, axis=0)
    total = jnp.sum(grid_gather(sq[None]), axis=0)
    return psi * lax.rsqrt(total / (rows * ngroups) + 1e-06)


def body_spread(orbitals, potential, fitted, points):
    rows = orbitals.shape[0]
    block_width = orbitals.shape[1]
    nbands = lax.axis_size("band")
    ngroups = lax.axis_size("grid")
    total_orbitals = block_width * nbands
    valid_mask = points >= 0
    safe_idx = jnp.where(valid_mask, points, 0)
    psi = orbitals
    for step in range(ITERS):
        orbital_block = psi.astype(jnp.bfloat16)
        selected_points = jnp.where(
            valid_mask[:, None], orbital_block[safe_idx], jnp.zeros((), jnp.bfloat16)
        )
        collocation_matrix = lax.all_gather(selected_points, "grid", axis=0, tiled=True)
        product = lax.dot_general(
            collocation_matrix,
            orbital_block,
            (((1,), (1,)), ((), ())),
            preferred_element_type=jnp.float32,
        )
        proj = lax.psum_scatter(
            (product / total_orbitals).astype(jnp.bfloat16), "band", scatter_dimension=0, tiled=True
        ).astype(jnp.float32)
        tile_blocks = (fitted.astype(jnp.float32) * proj).astype(jnp.bfloat16)
        orbitals_at_slots = lax.all_to_all(
            collocation_matrix, "band", split_axis=0, concat_axis=1, tiled=True
        )
        partial_value = lax.dot_general(
            tile_blocks,
            orbitals_at_slots,
            (((0,), (0,)), ((), ())),
            preferred_element_type=jnp.float32,
        )
        applied = lax.psum_scatter(
            partial_value.astype(jnp.bfloat16), "band", scatter_dimension=1, tiled=True
        ).astype(jnp.float32)
        fresh = psi - 0.25 * (potential[:, None] * psi - applied)
        squares = lax.psum(jnp.sum(fresh * fresh, axis=0), "grid")
        psi = fresh * lax.rsqrt(squares / (rows * ngroups) + 1e-06)
    return psi


def solution(mesh):
    in_specs = (P("grid", "band"), P("grid"), P("band", "grid"), P("grid"))
    out_specs = P("grid", "band")
    return jax.shard_map(body, mesh=mesh, in_specs=in_specs, out_specs=out_specs, check_vma=False)
```

```python
import jax
import jax.numpy as jnp
from jax import lax
from jax.sharding import PartitionSpec as P

ITERS = 2


def grid_copies(x):
    ngroups = lax.axis_size("grid")
    return jnp.broadcast_to(x[None], (ngroups,) + x.shape)


def grid_exchange(sent):
    got = lax.all_to_all(sent, "grid", 0, 0, tiled=True)
    return got.reshape((sent.shape[0] * sent.shape[1],) + sent.shape[2:])


def grid_gather(x):
    return grid_exchange(grid_copies(x))


def band_swap(x):
    nbands = lax.axis_size("band")
    got = [x]
    for k in range(1, nbands):
        got.append(lax.ppermute(x, "band", [(i, i ^ k) for i in range(nbands)]))
    return got


def pair_up(slots):
    ngroups, nslots = slots.shape[:2]
    pairs = slots.reshape((ngroups // 2, 2) + slots.shape[1:])
    return (pairs[:, 0] + jnp.flip(pairs[:, 1], axis=1)).reshape((ngroups // 2 * nslots,) + slots.shape[2:])


def band_hops(x):
    nbands = lax.axis_size("band")
    held = {0: x}
    bit = nbands // 2
    while bit:
        keys = sorted(held)
        got = lax.ppermute(jnp.concatenate([held[k] for k in keys], 0), "band", [(i, i ^ bit) for i in range(nbands)])
        for n, k in enumerate(keys):
            held[k ^ bit] = got[n * x.shape[0]:(n + 1) * x.shape[0]]
        bit //= 2
    return [held[k] for k in range(nbands)]


def body(orbitals, potential, fitted, points):
    ngroups = lax.axis_size("grid")
    nbands = lax.axis_size("band")
    nslots = points.shape[0]
    block_width = orbitals.shape[1]
    if ngroups > 8 or ngroups % 2 or nbands & (nbands - 1) or nslots > block_width:
        return body_spread(orbitals, potential, fitted, points)
    rows = orbitals.shape[0]
    band = lax.axis_index("band")
    total_orbitals = block_width * nbands
    valid_mask = points >= 0
    picks = (points[:, None] == jnp.arange(rows, dtype=points.dtype)[None, :]).astype(jnp.bfloat16)
    rows_b16 = orbitals.astype(jnp.bfloat16)
    selected = jnp.dot(picks, rows_b16, preferred_element_type=jnp.float32).astype(jnp.bfloat16)
    filled = jnp.pad(valid_mask.astype(jnp.bfloat16), (0, block_width - nslots))
    to_band = jnp.concatenate([rows_b16, fitted.reshape(-1, block_width)], 0)
    sent, to_band = lax.optimization_barrier((grid_copies(jnp.concatenate([selected, filled[None]], 0)), to_band))
    got = grid_exchange(sent).reshape(ngroups, nslots + 1, block_width)
    swapped = band_hops(to_band)
    rows_b = jnp.concatenate([part[:rows] for part in swapped], 1)
    fitted_got = jnp.stack([part[rows:].reshape(fitted.shape) for part in swapped], 0)
    fitted_all = jnp.take(fitted_got, jnp.arange(nbands, dtype=jnp.int32) ^ band, axis=0)
    fitted_all = fitted_all.reshape(ngroups // 2, 2, nslots, fitted.shape[1])
    coll = jnp.concatenate(band_hops(pair_up(got[:, :nslots])), 1)
    first_filled = got[:, nslots, :nslots].reshape(ngroups // 2, 2, nslots)[:, 0] > 0
    fitted_all = jnp.where(
        first_filled[:, :, None], fitted_all[:, 0], jnp.flip(fitted_all[:, 1], axis=1)
    ).reshape(-1, fitted.shape[1]).astype(jnp.float32)
    psi = orbitals
    pot = potential[:, None]
    for step in range(ITERS):
        if step:
            at_slots = jnp.dot(picks, psi, preferred_element_type=jnp.float32).astype(jnp.bfloat16)
            high = lax.reduce_precision(sq, exponent_bits=8, mantissa_bits=7)
            rest = sq - high
            middle = lax.reduce_precision(rest, exponent_bits=8, mantissa_bits=7)
            low = lax.reduce_precision(rest - middle, exponent_bits=8, mantissa_bits=7)
            parts = jnp.stack([high, middle, low], 0).astype(jnp.bfloat16)
            got = grid_gather(jnp.concatenate([at_slots, parts], 0)).reshape(ngroups, nslots + 3, block_width)
            sums = got[:, nslots:].astype(jnp.float32)
            total = jnp.sum((sums[:, 0] + sums[:, 1]) + sums[:, 2], axis=0)
            scale = lax.rsqrt(total / (rows * ngroups) + 1e-06)
            coll_own = pair_up((got[:, :nslots].astype(jnp.float32) * scale).astype(jnp.bfloat16))
            psi = psi * scale
            ncoll = coll_own.shape[0]
            swapped = band_hops(jnp.concatenate([coll_own, psi.astype(jnp.bfloat16)], 0))
            coll = jnp.concatenate([part[:ncoll] for part in swapped], 1)
            rows_b = jnp.concatenate([part[ncoll:] for part in swapped], 1)
        proj = None
        for k in range(nbands):
            part = lax.dot_general(
                coll[:, k * block_width:(k + 1) * block_width],
                rows_b[:, k * block_width:(k + 1) * block_width],
                (((1,), (1,)), ((), ())),
                preferred_element_type=jnp.float32,
            )
            part = (part / total_orbitals).astype(jnp.bfloat16).astype(jnp.float32)
            proj = part if proj is None else proj + part
        tile_blocks = (fitted_all * proj).astype(jnp.bfloat16)
        applied = lax.dot_general(
            tile_blocks, coll[:, :block_width], (((0,), (0,)), ((), ())), preferred_element_type=jnp.float32
        )
        psi = psi - 0.25 * (pot * psi - applied)
        sq = jnp.sum(psi * psi, axis=0)
    total = jnp.sum(grid_gather(sq[None]), axis=0)
    return psi * lax.rsqrt(total / (rows * ngroups) + 1e-06)


def body_spread(orbitals, potential, fitted, points):
    rows = orbitals.shape[0]
    block_width = orbitals.shape[1]
    nbands = lax.axis_size("band")
    ngroups = lax.axis_size("grid")
    total_orbitals = block_width * nbands
    valid_mask = points >= 0
    safe_idx = jnp.where(valid_mask, points, 0)
    psi = orbitals
    for step in range(ITERS):
        orbital_block = psi.astype(jnp.bfloat16)
        selected_points = jnp.where(
            valid_mask[:, None], orbital_block[safe_idx], jnp.zeros((), jnp.bfloat16)
        )
        collocation_matrix = lax.all_gather(selected_points, "grid", axis=0, tiled=True)
        product = lax.dot_general(
            collocation_matrix,
            orbital_block,
            (((1,), (1,)), ((), ())),
            preferred_element_type=jnp.float32,
        )
        proj = lax.psum_scatter(
            (product / total_orbitals).astype(jnp.bfloat16), "band", scatter_dimension=0, tiled=True
        ).astype(jnp.float32)
        tile_blocks = (fitted.astype(jnp.float32) * proj).astype(jnp.bfloat16)
        orbitals_at_slots = lax.all_to_all(
            collocation_matrix, "band", split_axis=0, concat_axis=1, tiled=True
        )
        partial_value = lax.dot_general(
            tile_blocks,
            orbitals_at_slots,
            (((0,), (0,)), ((), ())),
            preferred_element_type=jnp.float32,
        )
        applied = lax.psum_scatter(
            partial_value.astype(jnp.bfloat16), "band", scatter_dimension=1, tiled=True
        ).astype(jnp.float32)
        fresh = psi - 0.25 * (potential[:, None] * psi - applied)
        squares = lax.psum(jnp.sum(fresh * fresh, axis=0), "grid")
        psi = fresh * lax.rsqrt(squares / (rows * ngroups) + 1e-06)
    return psi


def solution(mesh):
    in_specs = (P("grid", "band"), P("grid"), P("band", "grid"), P("grid"))
    out_specs = P("grid", "band")
    return jax.shard_map(body, mesh=mesh, in_specs=in_specs, out_specs=out_specs, check_vma=False)
```

```python
import jax
import jax.numpy as jnp
from jax import lax
from jax.sharding import PartitionSpec as P

ITERS = 2


def grid_copies(x):
    ngroups = lax.axis_size("grid")
    return jnp.broadcast_to(x[None], (ngroups,) + x.shape)


def grid_exchange(sent):
    got = lax.all_to_all(sent, "grid", 0, 0, tiled=True)
    return got.reshape((sent.shape[0] * sent.shape[1],) + sent.shape[2:])


def grid_gather(x):
    return grid_exchange(grid_copies(x))


def band_swap(x):
    nbands = lax.axis_size("band")
    got = [x]
    for k in range(1, nbands):
        got.append(lax.ppermute(x, "band", [(i, i ^ k) for i in range(nbands)]))
    return got


def pair_up(slots):
    ngroups, nslots = slots.shape[:2]
    pairs = slots.reshape((ngroups // 2, 2) + slots.shape[1:])
    return (pairs[:, 0] + jnp.flip(pairs[:, 1], axis=1)).reshape((ngroups // 2 * nslots,) + slots.shape[2:])


def band_hops(x):
    nbands = lax.axis_size("band")
    held = {0: x}
    bit = nbands // 2
    while bit:
        keys = sorted(held)
        got = lax.ppermute(jnp.concatenate([held[k] for k in keys], 0), "band", [(i, i ^ bit) for i in range(nbands)])
        for n, k in enumerate(keys):
            held[k ^ bit] = got[n * x.shape[0]:(n + 1) * x.shape[0]]
        bit //= 2
    return [held[k] for k in range(nbands)]


def body(orbitals, potential, fitted, points):
    ngroups = lax.axis_size("grid")
    nbands = lax.axis_size("band")
    nslots = points.shape[0]
    block_width = orbitals.shape[1]
    if ngroups > 8 or ngroups % 2 or nbands & (nbands - 1) or nslots > block_width:
        return body_spread(orbitals, potential, fitted, points)
    rows = orbitals.shape[0]
    band = lax.axis_index("band")
    total_orbitals = block_width * nbands
    valid_mask = points >= 0
    picks = (points[:, None] == jnp.arange(rows, dtype=points.dtype)[None, :]).astype(jnp.bfloat16)
    rows_b16 = orbitals.astype(jnp.bfloat16)
    selected = jnp.dot(picks, rows_b16, preferred_element_type=jnp.float32).astype(jnp.bfloat16)
    filled = jnp.pad(valid_mask.astype(jnp.bfloat16), (0, block_width - nslots))
    to_band = jnp.concatenate([rows_b16, fitted.reshape(-1, block_width)], 0)
    sent, to_band = lax.optimization_barrier((grid_copies(jnp.concatenate([selected, filled[None]], 0)), to_band))
    got = grid_exchange(sent).reshape(ngroups, nslots + 1, block_width)
    swapped = band_hops(to_band)
    rows_b = jnp.concatenate([part[:rows] for part in swapped], 1)
    fitted_got = jnp.stack([part[rows:].reshape(fitted.shape) for part in swapped], 0)
    fitted_all = jnp.take(fitted_got, jnp.arange(nbands, dtype=jnp.int32) ^ band, axis=0)
    fitted_all = fitted_all.reshape(ngroups // 2, 2, nslots, fitted.shape[1])
    coll = jnp.concatenate(band_swap(pair_up(got[:, :nslots])), 1)
    first_filled = got[:, nslots, :nslots].reshape(ngroups // 2, 2, nslots)[:, 0] > 0
    fitted_all = jnp.where(
        first_filled[:, :, None], fitted_all[:, 0], jnp.flip(fitted_all[:, 1], axis=1)
    ).reshape(-1, fitted.shape[1]).astype(jnp.float32)
    psi = orbitals
    pot = potential[:, None]
    for step in range(ITERS):
        if step:
            at_slots = jnp.dot(picks, psi, preferred_element_type=jnp.float32).astype(jnp.bfloat16)
            high = lax.reduce_precision(sq, exponent_bits=8, mantissa_bits=7)
            rest = sq - high
            middle = lax.reduce_precision(rest, exponent_bits=8, mantissa_bits=7)
            low = lax.reduce_precision(rest - middle, exponent_bits=8, mantissa_bits=7)
            parts = jnp.stack([high, middle, low], 0).astype(jnp.bfloat16)
            got = grid_gather(jnp.concatenate([at_slots, parts], 0)).reshape(ngroups, nslots + 3, block_width)
            sums = got[:, nslots:].astype(jnp.float32)
            total = jnp.sum((sums[:, 0] + sums[:, 1]) + sums[:, 2], axis=0)
            scale = lax.rsqrt(total / (rows * ngroups) + 1e-06)
            coll_own = pair_up((got[:, :nslots].astype(jnp.float32) * scale).astype(jnp.bfloat16))
            psi = psi * scale
            ncoll = coll_own.shape[0]
            swapped = band_hops(jnp.concatenate([coll_own, psi.astype(jnp.bfloat16)], 0))
            coll = jnp.concatenate([part[:ncoll] for part in swapped], 1)
            rows_b = jnp.concatenate([part[ncoll:] for part in swapped], 1)
        proj = None
        for k in range(nbands):
            part = lax.dot_general(
                coll[:, k * block_width:(k + 1) * block_width],
                rows_b[:, k * block_width:(k + 1) * block_width],
                (((1,), (1,)), ((), ())),
                preferred_element_type=jnp.float32,
            )
            part = (part / total_orbitals).astype(jnp.bfloat16).astype(jnp.float32)
            proj = part if proj is None else proj + part
        tile_blocks = (fitted_all * proj).astype(jnp.bfloat16)
        applied = lax.dot_general(
            tile_blocks, coll[:, :block_width], (((0,), (0,)), ((), ())), preferred_element_type=jnp.float32
        )
        psi = psi - 0.25 * (pot * psi - applied)
        sq = jnp.sum(psi * psi, axis=0)
    total = jnp.sum(grid_gather(sq[None]), axis=0)
    return psi * lax.rsqrt(total / (rows * ngroups) + 1e-06)


def body_spread(orbitals, potential, fitted, points):
    rows = orbitals.shape[0]
    block_width = orbitals.shape[1]
    nbands = lax.axis_size("band")
    ngroups = lax.axis_size("grid")
    total_orbitals = block_width * nbands
    valid_mask = points >= 0
    safe_idx = jnp.where(valid_mask, points, 0)
    psi = orbitals
    for step in range(ITERS):
        orbital_block = psi.astype(jnp.bfloat16)
        selected_points = jnp.where(
            valid_mask[:, None], orbital_block[safe_idx], jnp.zeros((), jnp.bfloat16)
        )
        collocation_matrix = lax.all_gather(selected_points, "grid", axis=0, tiled=True)
        product = lax.dot_general(
            collocation_matrix,
            orbital_block,
            (((1,), (1,)), ((), ())),
            preferred_element_type=jnp.float32,
        )
        proj = lax.psum_scatter(
            (product / total_orbitals).astype(jnp.bfloat16), "band", scatter_dimension=0, tiled=True
        ).astype(jnp.float32)
        tile_blocks = (fitted.astype(jnp.float32) * proj).astype(jnp.bfloat16)
        orbitals_at_slots = lax.all_to_all(
            collocation_matrix, "band", split_axis=0, concat_axis=1, tiled=True
        )
        partial_value = lax.dot_general(
            tile_blocks,
            orbitals_at_slots,
            (((0,), (0,)), ((), ())),
            preferred_element_type=jnp.float32,
        )
        applied = lax.psum_scatter(
            partial_value.astype(jnp.bfloat16), "band", scatter_dimension=1, tiled=True
        ).astype(jnp.float32)
        fresh = psi - 0.25 * (potential[:, None] * psi - applied)
        squares = lax.psum(jnp.sum(fresh * fresh, axis=0), "grid")
        psi = fresh * lax.rsqrt(squares / (rows * ngroups) + 1e-06)
    return psi


def solution(mesh):
    in_specs = (P("grid", "band"), P("grid"), P("band", "grid"), P("grid"))
    out_specs = P("grid", "band")
    return jax.shard_map(body, mesh=mesh, in_specs=in_specs, out_specs=out_specs, check_vma=False)
```

```python
import jax
import jax.numpy as jnp
from jax import lax
from jax.sharding import PartitionSpec as P

ITERS = 2


def grid_copies(x):
    ngroups = lax.axis_size("grid")
    return jnp.broadcast_to(x[None], (ngroups,) + x.shape)


def grid_exchange(sent):
    got = lax.all_to_all(sent, "grid", 0, 0, tiled=True)
    return got.reshape((sent.shape[0] * sent.shape[1],) + sent.shape[2:])


def grid_gather(x):
    return grid_exchange(grid_copies(x))


def band_swap(x):
    nbands = lax.axis_size("band")
    got = [x]
    for k in range(1, nbands):
        got.append(lax.ppermute(x, "band", [(i, i ^ k) for i in range(nbands)]))
    return got


def pair_up(slots):
    ngroups, nslots = slots.shape[:2]
    pairs = slots.reshape((ngroups // 2, 2) + slots.shape[1:])
    return (pairs[:, 0] + jnp.flip(pairs[:, 1], axis=1)).reshape((ngroups // 2 * nslots,) + slots.shape[2:])


def band_hops(x):
    nbands = lax.axis_size("band")
    held = {0: x}
    bit = nbands // 2
    while bit:
        keys = sorted(held)
        got = lax.ppermute(jnp.concatenate([held[k] for k in keys], 0), "band", [(i, i ^ bit) for i in range(nbands)])
        for n, k in enumerate(keys):
            held[k ^ bit] = got[n * x.shape[0]:(n + 1) * x.shape[0]]
        bit //= 2
    return [held[k] for k in range(nbands)]


def body(orbitals, potential, fitted, points):
    ngroups = lax.axis_size("grid")
    nbands = lax.axis_size("band")
    nslots = points.shape[0]
    block_width = orbitals.shape[1]
    if ngroups > 8 or ngroups % 2 or nbands & (nbands - 1) or nslots > block_width:
        return body_spread(orbitals, potential, fitted, points)
    rows = orbitals.shape[0]
    band = lax.axis_index("band")
    total_orbitals = block_width * nbands
    valid_mask = points >= 0
    picks = (points[:, None] == jnp.arange(rows, dtype=points.dtype)[None, :]).astype(jnp.bfloat16)
    selected = jnp.dot(picks, orbitals, preferred_element_type=jnp.float32).astype(jnp.bfloat16)
    filled = jnp.pad(valid_mask.astype(jnp.bfloat16), (0, block_width - nslots))
    sent = lax.optimization_barrier(grid_copies(jnp.concatenate([selected, filled[None]], 0)))
    got = grid_exchange(sent).reshape(ngroups, nslots + 1, block_width)
    to_band = jnp.concatenate([orbitals.astype(jnp.bfloat16), fitted.reshape(-1, block_width)], 0)
    pot = potential[:, None]
    got, first_pot_psi = lax.optimization_barrier((got, pot * orbitals))
    swapped = band_hops(to_band)
    rows_b = jnp.concatenate([part[:rows] for part in swapped], 1)
    fitted_got = jnp.stack([part[rows:].reshape(fitted.shape) for part in swapped], 0)
    fitted_all = jnp.take(fitted_got, jnp.arange(nbands, dtype=jnp.int32) ^ band, axis=0)
    fitted_all = fitted_all.reshape(ngroups // 2, 2, nslots, fitted.shape[1])
    coll = jnp.concatenate(band_hops(pair_up(got[:, :nslots])), 1)
    first_filled = got[:, nslots, :nslots].reshape(ngroups // 2, 2, nslots)[:, 0] > 0
    fitted_all = jnp.where(
        first_filled[:, :, None], fitted_all[:, 0], jnp.flip(fitted_all[:, 1], axis=1)
    ).reshape(-1, fitted.shape[1]).astype(jnp.float32)
    psi = orbitals
    for step in range(ITERS):
        if step:
            at_slots = jnp.dot(picks, psi, preferred_element_type=jnp.float32).astype(jnp.bfloat16)
            high = lax.reduce_precision(sq, exponent_bits=8, mantissa_bits=7)
            rest = sq - high
            middle = lax.reduce_precision(rest, exponent_bits=8, mantissa_bits=7)
            low = lax.reduce_precision(rest - middle, exponent_bits=8, mantissa_bits=7)
            parts = jnp.stack([high, middle, low], 0).astype(jnp.bfloat16)
            got = grid_gather(jnp.concatenate([at_slots, parts], 0)).reshape(ngroups, nslots + 3, block_width)
            sums = got[:, nslots:].astype(jnp.float32)
            total = jnp.sum((sums[:, 0] + sums[:, 1]) + sums[:, 2], axis=0)
            scale = lax.rsqrt(total / (rows * ngroups) + 1e-06)
            coll_own = pair_up((got[:, :nslots].astype(jnp.float32) * scale).astype(jnp.bfloat16))
            psi = psi * scale
            ncoll = coll_own.shape[0]
            swapped = band_hops(jnp.concatenate([coll_own, psi.astype(jnp.bfloat16)], 0))
            coll = jnp.concatenate([part[:ncoll] for part in swapped], 1)
            rows_b = jnp.concatenate([part[ncoll:] for part in swapped], 1)
        proj = None
        for k in range(nbands):
            part = lax.dot_general(
                coll[:, k * block_width:(k + 1) * block_width],
                rows_b[:, k * block_width:(k + 1) * block_width],
                (((1,), (1,)), ((), ())),
                preferred_element_type=jnp.float32,
            )
            part = (part / total_orbitals).astype(jnp.bfloat16).astype(jnp.float32)
            proj = part if proj is None else proj + part
        tile_blocks = (fitted_all * proj).astype(jnp.bfloat16)
        applied = lax.dot_general(
            tile_blocks, coll[:, :block_width], (((0,), (0,)), ((), ())), preferred_element_type=jnp.float32
        )
        pot_psi = first_pot_psi if step == 0 else pot * psi
        psi = psi - 0.25 * (pot_psi - applied)
        sq = jnp.sum(psi * psi, axis=0)
    total = jnp.sum(grid_gather(sq[None]), axis=0)
    return psi * lax.rsqrt(total / (rows * ngroups) + 1e-06)


def body_spread(orbitals, potential, fitted, points):
    rows = orbitals.shape[0]
    block_width = orbitals.shape[1]
    nbands = lax.axis_size("band")
    ngroups = lax.axis_size("grid")
    total_orbitals = block_width * nbands
    valid_mask = points >= 0
    safe_idx = jnp.where(valid_mask, points, 0)
    psi = orbitals
    for step in range(ITERS):
        orbital_block = psi.astype(jnp.bfloat16)
        selected_points = jnp.where(
            valid_mask[:, None], orbital_block[safe_idx], jnp.zeros((), jnp.bfloat16)
        )
        collocation_matrix = lax.all_gather(selected_points, "grid", axis=0, tiled=True)
        product = lax.dot_general(
            collocation_matrix,
            orbital_block,
            (((1,), (1,)), ((), ())),
            preferred_element_type=jnp.float32,
        )
        proj = lax.psum_scatter(
            (product / total_orbitals).astype(jnp.bfloat16), "band", scatter_dimension=0, tiled=True
        ).astype(jnp.float32)
        tile_blocks = (fitted.astype(jnp.float32) * proj).astype(jnp.bfloat16)
        orbitals_at_slots = lax.all_to_all(
            collocation_matrix, "band", split_axis=0, concat_axis=1, tiled=True
        )
        partial_value = lax.dot_general(
            tile_blocks,
            orbitals_at_slots,
            (((0,), (0,)), ((), ())),
            preferred_element_type=jnp.float32,
        )
        applied = lax.psum_scatter(
            partial_value.astype(jnp.bfloat16), "band", scatter_dimension=1, tiled=True
        ).astype(jnp.float32)
        fresh = psi - 0.25 * (potential[:, None] * psi - applied)
        squares = lax.psum(jnp.sum(fresh * fresh, axis=0), "grid")
        psi = fresh * lax.rsqrt(squares / (rows * ngroups) + 1e-06)
    return psi


def solution(mesh):
    in_specs = (P("grid", "band"), P("grid"), P("band", "grid"), P("grid"))
    out_specs = P("grid", "band")
    return jax.shard_map(body, mesh=mesh, in_specs=in_specs, out_specs=out_specs, check_vma=False)
```

```python
import jax
import jax.numpy as jnp
from jax import lax
from jax.sharding import PartitionSpec as P

ITERS = 2


def grid_copies(x):
    ngroups = lax.axis_size("grid")
    return jnp.broadcast_to(x[None], (ngroups,) + x.shape)


def grid_exchange(sent):
    got = lax.all_to_all(sent, "grid", 0, 0, tiled=True)
    return got.reshape((sent.shape[0] * sent.shape[1],) + sent.shape[2:])


def grid_gather(x):
    return grid_exchange(grid_copies(x))


def band_swap(x):
    nbands = lax.axis_size("band")
    got = [x]
    for k in range(1, nbands):
        got.append(lax.ppermute(x, "band", [(i, i ^ k) for i in range(nbands)]))
    return got


def pair_up(slots):
    ngroups, nslots = slots.shape[:2]
    pairs = slots.reshape((ngroups // 2, 2) + slots.shape[1:])
    return (pairs[:, 0] + jnp.flip(pairs[:, 1], axis=1)).reshape((ngroups // 2 * nslots,) + slots.shape[2:])


def band_hops(x):
    nbands = lax.axis_size("band")
    held = {0: x}
    bit = nbands // 2
    while bit:
        keys = sorted(held)
        got = lax.ppermute(jnp.concatenate([held[k] for k in keys], 0), "band", [(i, i ^ bit) for i in range(nbands)])
        for n, k in enumerate(keys):
            held[k ^ bit] = got[n * x.shape[0]:(n + 1) * x.shape[0]]
        bit //= 2
    return [held[k] for k in range(nbands)]


def body(orbitals, potential, fitted, points):
    ngroups = lax.axis_size("grid")
    nbands = lax.axis_size("band")
    nslots = points.shape[0]
    block_width = orbitals.shape[1]
    if ngroups > 8 or ngroups % 2 or nbands & (nbands - 1) or nslots > block_width:
        return body_spread(orbitals, potential, fitted, points)
    rows = orbitals.shape[0]
    band = lax.axis_index("band")
    total_orbitals = block_width * nbands
    valid_mask = points >= 0
    picks = (points[:, None] == jnp.arange(rows, dtype=points.dtype)[None, :]).astype(jnp.bfloat16)
    rows_b16 = orbitals.astype(jnp.bfloat16)
    selected = jnp.dot(picks, rows_b16, preferred_element_type=jnp.float32).astype(jnp.bfloat16)
    filled = jnp.pad(valid_mask.astype(jnp.bfloat16), (0, block_width - nslots))
    to_band = jnp.concatenate([rows_b16, fitted.reshape(-1, block_width)], 0)
    sent, to_band = lax.optimization_barrier((grid_copies(jnp.concatenate([selected, filled[None]], 0)), to_band))
    got = grid_exchange(sent).reshape(ngroups, nslots + 1, block_width)
    swapped = band_hops(to_band)
    rows_b = jnp.concatenate([part[:rows] for part in swapped], 1)
    fitted_got = jnp.stack([part[rows:].reshape(fitted.shape) for part in swapped], 0)
    fitted_all = jnp.take(fitted_got, jnp.arange(nbands, dtype=jnp.int32) ^ band, axis=0)
    fitted_all = fitted_all.reshape(ngroups // 2, 2, nslots, fitted.shape[1])
    coll = jnp.concatenate(band_hops(pair_up(got[:, :nslots])), 1)
    first_filled = got[:, nslots, :nslots].reshape(ngroups // 2, 2, nslots)[:, 0] > 0
    fitted_all = jnp.where(
        first_filled[:, :, None], fitted_all[:, 0], jnp.flip(fitted_all[:, 1], axis=1)
    ).reshape(-1, fitted.shape[1]).astype(jnp.float32)
    psi = orbitals
    pot = potential[:, None]
    for step in range(ITERS):
        if step:
            fresh_swapped = band_hops(psi)
            at_slots = jnp.dot(picks, psi, preferred_element_type=jnp.float32).astype(jnp.bfloat16)
            high = lax.reduce_precision(sq, exponent_bits=8, mantissa_bits=7)
            rest = sq - high
            middle = lax.reduce_precision(rest, exponent_bits=8, mantissa_bits=7)
            low = lax.reduce_precision(rest - middle, exponent_bits=8, mantissa_bits=7)
            parts = jnp.stack([high, middle, low], 0).astype(jnp.bfloat16)
            got = grid_gather(jnp.concatenate([at_slots, parts], 0)).reshape(ngroups, nslots + 3, block_width)
            sums = got[:, nslots:].astype(jnp.float32)
            total = jnp.sum((sums[:, 0] + sums[:, 1]) + sums[:, 2], axis=0)
            scale = lax.rsqrt(total / (rows * ngroups) + 1e-06)
            coll_own = pair_up((got[:, :nslots].astype(jnp.float32) * scale).astype(jnp.bfloat16))
            ncoll = coll_own.shape[0]
            high = lax.reduce_precision(scale, exponent_bits=8, mantissa_bits=7)
            rest = scale - high
            middle = lax.reduce_precision(rest, exponent_bits=8, mantissa_bits=7)
            low = lax.reduce_precision(rest - middle, exponent_bits=8, mantissa_bits=7)
            scale_parts = jnp.stack([high, middle, low], 0).astype(jnp.bfloat16)
            swapped = band_hops(jnp.concatenate([coll_own, scale_parts], 0))
            coll = jnp.concatenate([part[:ncoll] for part in swapped], 1)
            scaled = []
            for part, fresh_rows in zip(swapped, fresh_swapped):
                got_scale = part[ncoll:].astype(jnp.float32)
                scaled.append((fresh_rows * ((got_scale[0] + got_scale[1]) + got_scale[2])).astype(jnp.bfloat16))
            rows_b = jnp.concatenate(scaled, 1)
            psi = psi * scale
        proj = None
        for k in range(nbands):
            part = lax.dot_general(
                coll[:, k * block_width:(k + 1) * block_width],
                rows_b[:, k * block_width:(k + 1) * block_width],
                (((1,), (1,)), ((), ())),
                preferred_element_type=jnp.float32,
            )
            part = (part / total_orbitals).astype(jnp.bfloat16).astype(jnp.float32)
            proj = part if proj is None else proj + part
        tile_blocks = (fitted_all * proj).astype(jnp.bfloat16)
        applied = lax.dot_general(
            tile_blocks, coll[:, :block_width], (((0,), (0,)), ((), ())), preferred_element_type=jnp.float32
        )
        psi = psi - 0.25 * (pot * psi - applied)
        sq = jnp.sum(psi * psi, axis=0)
    total = jnp.sum(grid_gather(sq[None]), axis=0)
    return psi * lax.rsqrt(total / (rows * ngroups) + 1e-06)


def body_spread(orbitals, potential, fitted, points):
    rows = orbitals.shape[0]
    block_width = orbitals.shape[1]
    nbands = lax.axis_size("band")
    ngroups = lax.axis_size("grid")
    total_orbitals = block_width * nbands
    valid_mask = points >= 0
    safe_idx = jnp.where(valid_mask, points, 0)
    psi = orbitals
    for step in range(ITERS):
        orbital_block = psi.astype(jnp.bfloat16)
        selected_points = jnp.where(
            valid_mask[:, None], orbital_block[safe_idx], jnp.zeros((), jnp.bfloat16)
        )
        collocation_matrix = lax.all_gather(selected_points, "grid", axis=0, tiled=True)
        product = lax.dot_general(
            collocation_matrix,
            orbital_block,
            (((1,), (1,)), ((), ())),
            preferred_element_type=jnp.float32,
        )
        proj = lax.psum_scatter(
            (product / total_orbitals).astype(jnp.bfloat16), "band", scatter_dimension=0, tiled=True
        ).astype(jnp.float32)
        tile_blocks = (fitted.astype(jnp.float32) * proj).astype(jnp.bfloat16)
        orbitals_at_slots = lax.all_to_all(
            collocation_matrix, "band", split_axis=0, concat_axis=1, tiled=True
        )
        partial_value = lax.dot_general(
            tile_blocks,
            orbitals_at_slots,
            (((0,), (0,)), ((), ())),
            preferred_element_type=jnp.float32,
        )
        applied = lax.psum_scatter(
            partial_value.astype(jnp.bfloat16), "band", scatter_dimension=1, tiled=True
        ).astype(jnp.float32)
        fresh = psi - 0.25 * (potential[:, None] * psi - applied)
        squares = lax.psum(jnp.sum(fresh * fresh, axis=0), "grid")
        psi = fresh * lax.rsqrt(squares / (rows * ngroups) + 1e-06)
    return psi


def solution(mesh):
    in_specs = (P("grid", "band"), P("grid"), P("band", "grid"), P("grid"))
    out_specs = P("grid", "band")
    return jax.shard_map(body, mesh=mesh, in_specs=in_specs, out_specs=out_specs, check_vma=False)
```

```python
import jax
import jax.numpy as jnp
from jax import lax
from jax.sharding import PartitionSpec as P

ITERS = 2


def grid_copies(x):
    ngroups = lax.axis_size("grid")
    return jnp.broadcast_to(x[None], (ngroups,) + x.shape)


def grid_exchange(sent):
    got = lax.all_to_all(sent, "grid", 0, 0, tiled=True)
    return got.reshape((sent.shape[0] * sent.shape[1],) + sent.shape[2:])


def grid_gather(x):
    return grid_exchange(grid_copies(x))


def band_swap(x):
    nbands = lax.axis_size("band")
    got = [x]
    for k in range(1, nbands):
        got.append(lax.ppermute(x, "band", [(i, i ^ k) for i in range(nbands)]))
    return got


def pair_up(slots):
    ngroups, nslots = slots.shape[:2]
    pairs = slots.reshape((ngroups // 2, 2) + slots.shape[1:])
    return (pairs[:, 0] + jnp.flip(pairs[:, 1], axis=1)).reshape((ngroups // 2 * nslots,) + slots.shape[2:])


def band_hops(x):
    nbands = lax.axis_size("band")
    held = {0: x}
    bit = nbands // 2
    while bit:
        keys = sorted(held)
        got = lax.ppermute(jnp.concatenate([held[k] for k in keys], 0), "band", [(i, i ^ bit) for i in range(nbands)])
        for n, k in enumerate(keys):
            held[k ^ bit] = got[n * x.shape[0]:(n + 1) * x.shape[0]]
        bit //= 2
    return [held[k] for k in range(nbands)]


def tree_gather(slots, extra, merge_first, merge_extra):
    ngroups = lax.axis_size("grid")
    g = lax.axis_index("grid")
    nslots = slots.shape[0]
    got = lax.ppermute(jnp.concatenate([slots, extra], 0), "grid", [(i, i ^ 1) for i in range(ngroups)])
    lower = (g & 1) == 1
    first = jnp.where(lower, got[:nslots], slots)
    second = jnp.where(lower, slots, got[:nslots])
    cur = first + jnp.flip(second, axis=0)
    extra = merge_first(extra, got[nslots:], lower)
    step = 2
    while step < ngroups:
        got = lax.ppermute(jnp.concatenate([cur, extra], 0), "grid", [(i, i ^ step) for i in range(ngroups)])
        lower = (g & step) != 0
        n = cur.shape[0]
        cur = jnp.where(lower, jnp.concatenate([got[:n], cur], 0), jnp.concatenate([cur, got[:n]], 0))
        extra = merge_extra(extra, got[n:], lower)
        step *= 2
    return cur, extra


def pick_first(own, got, lower):
    return jnp.where(lower, got, own)


def in_order(own, got, lower):
    return jnp.where(lower, jnp.concatenate([got, own], 0), jnp.concatenate([own, got], 0))


def body(orbitals, potential, fitted, points):
    ngroups = lax.axis_size("grid")
    nbands = lax.axis_size("band")
    nslots = points.shape[0]
    block_width = orbitals.shape[1]
    if ngroups > 8 or ngroups & (ngroups - 1) or nbands & (nbands - 1) or nslots > block_width:
        return body_spread(orbitals, potential, fitted, points)
    rows = orbitals.shape[0]
    band = lax.axis_index("band")
    total_orbitals = block_width * nbands
    valid_mask = points >= 0
    picks = (points[:, None] == jnp.arange(rows, dtype=points.dtype)[None, :]).astype(jnp.bfloat16)
    rows_b16 = orbitals.astype(jnp.bfloat16)
    selected = jnp.dot(picks, rows_b16, preferred_element_type=jnp.float32).astype(jnp.bfloat16)
    filled = jnp.pad(valid_mask.astype(jnp.bfloat16), (0, block_width - nslots))
    to_band = jnp.concatenate([rows_b16, fitted.reshape(-1, block_width)], 0)
    sel, mask_row, to_band = lax.optimization_barrier((selected, filled[None], to_band))
    merged, first_rows = tree_gather(sel, mask_row, pick_first, in_order)
    swapped = band_hops(to_band)
    rows_b = jnp.concatenate([part[:rows] for part in swapped], 1)
    fitted_got = jnp.stack([part[rows:].reshape(fitted.shape) for part in swapped], 0)
    fitted_all = jnp.take(fitted_got, jnp.arange(nbands, dtype=jnp.int32) ^ band, axis=0)
    fitted_all = fitted_all.reshape(ngroups // 2, 2, nslots, fitted.shape[1])
    coll = jnp.concatenate(band_hops(merged), 1)
    first_filled = first_rows[:, :nslots] > 0
    fitted_all = jnp.where(
        first_filled[:, :, None], fitted_all[:, 0], jnp.flip(fitted_all[:, 1], axis=1)
    ).reshape(-1, fitted.shape[1]).astype(jnp.float32)
    psi = orbitals
    pot = potential[:, None]
    for step in range(ITERS):
        if step:
            at_slots = jnp.dot(picks, psi, preferred_element_type=jnp.float32).astype(jnp.bfloat16)
            high = lax.reduce_precision(sq, exponent_bits=8, mantissa_bits=7)
            rest = sq - high
            middle = lax.reduce_precision(rest, exponent_bits=8, mantissa_bits=7)
            low = lax.reduce_precision(rest - middle, exponent_bits=8, mantissa_bits=7)
            parts = jnp.stack([high, middle, low], 0).astype(jnp.bfloat16)
            got = grid_gather(jnp.concatenate([at_slots, parts], 0)).reshape(ngroups, nslots + 3, block_width)
            sums = got[:, nslots:].astype(jnp.float32)
            total = jnp.sum((sums[:, 0] + sums[:, 1]) + sums[:, 2], axis=0)
            scale = lax.rsqrt(total / (rows * ngroups) + 1e-06)
            coll_own = pair_up((got[:, :nslots].astype(jnp.float32) * scale).astype(jnp.bfloat16))
            psi = psi * scale
            ncoll = coll_own.shape[0]
            swapped = band_hops(jnp.concatenate([coll_own, psi.astype(jnp.bfloat16)], 0))
            coll = jnp.concatenate([part[:ncoll] for part in swapped], 1)
            rows_b = jnp.concatenate([part[ncoll:] for part in swapped], 1)
        proj = None
        for k in range(nbands):
            part = lax.dot_general(
                coll[:, k * block_width:(k + 1) * block_width],
                rows_b[:, k * block_width:(k + 1) * block_width],
                (((1,), (1,)), ((), ())),
                preferred_element_type=jnp.float32,
            )
            part = (part / total_orbitals).astype(jnp.bfloat16).astype(jnp.float32)
            proj = part if proj is None else proj + part
        tile_blocks = (fitted_all * proj).astype(jnp.bfloat16)
        applied = lax.dot_general(
            tile_blocks, coll[:, :block_width], (((0,), (0,)), ((), ())), preferred_element_type=jnp.float32
        )
        psi = psi - 0.25 * (pot * psi - applied)
        sq = jnp.sum(psi * psi, axis=0)
    total = jnp.sum(grid_gather(sq[None]), axis=0)
    return psi * lax.rsqrt(total / (rows * ngroups) + 1e-06)


def body_spread(orbitals, potential, fitted, points):
    rows = orbitals.shape[0]
    block_width = orbitals.shape[1]
    nbands = lax.axis_size("band")
    ngroups = lax.axis_size("grid")
    total_orbitals = block_width * nbands
    valid_mask = points >= 0
    safe_idx = jnp.where(valid_mask, points, 0)
    psi = orbitals
    for step in range(ITERS):
        orbital_block = psi.astype(jnp.bfloat16)
        selected_points = jnp.where(
            valid_mask[:, None], orbital_block[safe_idx], jnp.zeros((), jnp.bfloat16)
        )
        collocation_matrix = lax.all_gather(selected_points, "grid", axis=0, tiled=True)
        product = lax.dot_general(
            collocation_matrix,
            orbital_block,
            (((1,), (1,)), ((), ())),
            preferred_element_type=jnp.float32,
        )
        proj = lax.psum_scatter(
            (product / total_orbitals).astype(jnp.bfloat16), "band", scatter_dimension=0, tiled=True
        ).astype(jnp.float32)
        tile_blocks = (fitted.astype(jnp.float32) * proj).astype(jnp.bfloat16)
        orbitals_at_slots = lax.all_to_all(
            collocation_matrix, "band", split_axis=0, concat_axis=1, tiled=True
        )
        partial_value = lax.dot_general(
            tile_blocks,
            orbitals_at_slots,
            (((0,), (0,)), ((), ())),
            preferred_element_type=jnp.float32,
        )
        applied = lax.psum_scatter(
            partial_value.astype(jnp.bfloat16), "band", scatter_dimension=1, tiled=True
        ).astype(jnp.float32)
        fresh = psi - 0.25 * (potential[:, None] * psi - applied)
        squares = lax.psum(jnp.sum(fresh * fresh, axis=0), "grid")
        psi = fresh * lax.rsqrt(squares / (rows * ngroups) + 1e-06)
    return psi


def solution(mesh):
    in_specs = (P("grid", "band"), P("grid"), P("band", "grid"), P("grid"))
    out_specs = P("grid", "band")
    return jax.shard_map(body, mesh=mesh, in_specs=in_specs, out_specs=out_specs, check_vma=False)
```

```python
import jax
import jax.numpy as jnp
from jax import lax
from jax.sharding import PartitionSpec as P

ITERS = 2


def grid_copies(x):
    ngroups = lax.axis_size("grid")
    return jnp.broadcast_to(x[None], (ngroups,) + x.shape)


def grid_exchange(sent):
    got = lax.all_to_all(sent, "grid", 0, 0, tiled=True)
    return got.reshape((sent.shape[0] * sent.shape[1],) + sent.shape[2:])


def grid_gather(x):
    return grid_exchange(grid_copies(x))


def band_swap(x):
    nbands = lax.axis_size("band")
    got = [x]
    for k in range(1, nbands):
        got.append(lax.ppermute(x, "band", [(i, i ^ k) for i in range(nbands)]))
    return got


def pair_up(slots):
    ngroups, nslots = slots.shape[:2]
    pairs = slots.reshape((ngroups // 2, 2) + slots.shape[1:])
    return (pairs[:, 0] + jnp.flip(pairs[:, 1], axis=1)).reshape((ngroups // 2 * nslots,) + slots.shape[2:])


def band_hops(x):
    nbands = lax.axis_size("band")
    held = {0: x}
    bit = nbands // 2
    while bit:
        keys = sorted(held)
        got = lax.ppermute(jnp.concatenate([held[k] for k in keys], 0), "band", [(i, i ^ bit) for i in range(nbands)])
        for n, k in enumerate(keys):
            held[k ^ bit] = got[n * x.shape[0]:(n + 1) * x.shape[0]]
        bit //= 2
    return [held[k] for k in range(nbands)]


def body(orbitals, potential, fitted, points):
    ngroups = lax.axis_size("grid")
    nbands = lax.axis_size("band")
    nslots = points.shape[0]
    block_width = orbitals.shape[1]
    if ngroups > 8 or ngroups % 2 or nbands & (nbands - 1) or nslots > block_width:
        return body_spread(orbitals, potential, fitted, points)
    rows = orbitals.shape[0]
    band = lax.axis_index("band")
    total_orbitals = block_width * nbands
    valid_mask = points >= 0
    picks = (points[:, None] == jnp.arange(rows, dtype=points.dtype)[None, :]).astype(jnp.bfloat16)
    rows_b16 = orbitals.astype(jnp.bfloat16)
    selected = jnp.dot(picks, rows_b16, preferred_element_type=jnp.float32).astype(jnp.bfloat16)
    filled = jnp.pad(valid_mask.astype(jnp.bfloat16), (0, block_width - nslots))
    to_band = jnp.concatenate([rows_b16, fitted.reshape(-1, block_width)], 0)
    sent, to_band = lax.optimization_barrier((grid_copies(jnp.concatenate([selected, filled[None]], 0)), to_band))
    got = grid_exchange(sent).reshape(ngroups, nslots + 1, block_width)
    pot = potential[:, None]
    got, first_pot_psi = lax.optimization_barrier((got, pot * orbitals))
    swapped = band_hops(to_band)
    rows_b = jnp.concatenate([part[:rows] for part in swapped], 1)
    fitted_got = jnp.stack([part[rows:].reshape(fitted.shape) for part in swapped], 0)
    fitted_all = jnp.take(fitted_got, jnp.arange(nbands, dtype=jnp.int32) ^ band, axis=0)
    fitted_all = fitted_all.reshape(ngroups // 2, 2, nslots, fitted.shape[1])
    coll = jnp.concatenate(band_hops(pair_up(got[:, :nslots])), 1)
    first_filled = got[:, nslots, :nslots].reshape(ngroups // 2, 2, nslots)[:, 0] > 0
    fitted_all = jnp.where(
        first_filled[:, :, None], fitted_all[:, 0], jnp.flip(fitted_all[:, 1], axis=1)
    ).reshape(-1, fitted.shape[1]).astype(jnp.float32)
    psi = orbitals
    for step in range(ITERS):
        if step:
            at_slots = jnp.dot(picks, psi, preferred_element_type=jnp.float32).astype(jnp.bfloat16)
            high = lax.reduce_precision(sq, exponent_bits=8, mantissa_bits=7)
            rest = sq - high
            middle = lax.reduce_precision(rest, exponent_bits=8, mantissa_bits=7)
            low = lax.reduce_precision(rest - middle, exponent_bits=8, mantissa_bits=7)
            parts = jnp.stack([high, middle, low], 0).astype(jnp.bfloat16)
            got = grid_gather(jnp.concatenate([at_slots, parts], 0)).reshape(ngroups, nslots + 3, block_width)
            sums = got[:, nslots:].astype(jnp.float32)
            total = jnp.sum((sums[:, 0] + sums[:, 1]) + sums[:, 2], axis=0)
            scale = lax.rsqrt(total / (rows * ngroups) + 1e-06)
            coll_own = pair_up((got[:, :nslots].astype(jnp.float32) * scale).astype(jnp.bfloat16))
            psi = psi * scale
            ncoll = coll_own.shape[0]
            swapped = band_hops(jnp.concatenate([coll_own, psi.astype(jnp.bfloat16)], 0))
            coll = jnp.concatenate([part[:ncoll] for part in swapped], 1)
            rows_b = jnp.concatenate([part[ncoll:] for part in swapped], 1)
        proj = None
        for k in range(nbands):
            part = lax.dot_general(
                coll[:, k * block_width:(k + 1) * block_width],
                rows_b[:, k * block_width:(k + 1) * block_width],
                (((1,), (1,)), ((), ())),
                preferred_element_type=jnp.float32,
            )
            part = (part / total_orbitals).astype(jnp.bfloat16).astype(jnp.float32)
            proj = part if proj is None else proj + part
        tile_blocks = (fitted_all * proj).astype(jnp.bfloat16)
        applied = lax.dot_general(
            tile_blocks, coll[:, :block_width], (((0,), (0,)), ((), ())), preferred_element_type=jnp.float32
        )
        pot_psi = first_pot_psi if step == 0 else pot * psi
        psi = psi - 0.25 * (pot_psi - applied)
        sq = jnp.sum(psi * psi, axis=0)
    total = jnp.sum(grid_gather(sq[None]), axis=0)
    return psi * lax.rsqrt(total / (rows * ngroups) + 1e-06)


def body_spread(orbitals, potential, fitted, points):
    rows = orbitals.shape[0]
    block_width = orbitals.shape[1]
    nbands = lax.axis_size("band")
    ngroups = lax.axis_size("grid")
    total_orbitals = block_width * nbands
    valid_mask = points >= 0
    safe_idx = jnp.where(valid_mask, points, 0)
    psi = orbitals
    for step in range(ITERS):
        orbital_block = psi.astype(jnp.bfloat16)
        selected_points = jnp.where(
            valid_mask[:, None], orbital_block[safe_idx], jnp.zeros((), jnp.bfloat16)
        )
        collocation_matrix = lax.all_gather(selected_points, "grid", axis=0, tiled=True)
        product = lax.dot_general(
            collocation_matrix,
            orbital_block,
            (((1,), (1,)), ((), ())),
            preferred_element_type=jnp.float32,
        )
        proj = lax.psum_scatter(
            (product / total_orbitals).astype(jnp.bfloat16), "band", scatter_dimension=0, tiled=True
        ).astype(jnp.float32)
        tile_blocks = (fitted.astype(jnp.float32) * proj).astype(jnp.bfloat16)
        orbitals_at_slots = lax.all_to_all(
            collocation_matrix, "band", split_axis=0, concat_axis=1, tiled=True
        )
        partial_value = lax.dot_general(
            tile_blocks,
            orbitals_at_slots,
            (((0,), (0,)), ((), ())),
            preferred_element_type=jnp.float32,
        )
        applied = lax.psum_scatter(
            partial_value.astype(jnp.bfloat16), "band", scatter_dimension=1, tiled=True
        ).astype(jnp.float32)
        fresh = psi - 0.25 * (potential[:, None] * psi - applied)
        squares = lax.psum(jnp.sum(fresh * fresh, axis=0), "grid")
        psi = fresh * lax.rsqrt(squares / (rows * ngroups) + 1e-06)
    return psi


def solution(mesh):
    in_specs = (P("grid", "band"), P("grid"), P("band", "grid"), P("grid"))
    out_specs = P("grid", "band")
    return jax.shard_map(body, mesh=mesh, in_specs=in_specs, out_specs=out_specs, check_vma=False)
```

```python
import jax
import jax.numpy as jnp
from jax import lax
from jax.sharding import PartitionSpec as P

ITERS = 2


def grid_copies(x):
    ngroups = lax.axis_size("grid")
    return jnp.broadcast_to(x[None], (ngroups,) + x.shape)


def grid_exchange(sent):
    got = lax.all_to_all(sent, "grid", 0, 0, tiled=True)
    return got.reshape((sent.shape[0] * sent.shape[1],) + sent.shape[2:])


def grid_gather(x):
    return grid_exchange(grid_copies(x))


def band_swap(x):
    nbands = lax.axis_size("band")
    got = [x]
    for k in range(1, nbands):
        got.append(lax.ppermute(x, "band", [(i, i ^ k) for i in range(nbands)]))
    return got


def pair_up(slots):
    ngroups, nslots = slots.shape[:2]
    pairs = slots.reshape((ngroups // 2, 2) + slots.shape[1:])
    return (pairs[:, 0] + jnp.flip(pairs[:, 1], axis=1)).reshape((ngroups // 2 * nslots,) + slots.shape[2:])


def band_hops(x):
    nbands = lax.axis_size("band")
    held = {0: x}
    bit = nbands // 2
    while bit:
        keys = sorted(held)
        got = lax.ppermute(jnp.concatenate([held[k] for k in keys], 0), "band", [(i, i ^ bit) for i in range(nbands)])
        for n, k in enumerate(keys):
            held[k ^ bit] = got[n * x.shape[0]:(n + 1) * x.shape[0]]
        bit //= 2
    return [held[k] for k in range(nbands)]


def body(orbitals, potential, fitted, points):
    ngroups = lax.axis_size("grid")
    nbands = lax.axis_size("band")
    nslots = points.shape[0]
    block_width = orbitals.shape[1]
    if ngroups > 8 or ngroups % 2 or nbands & (nbands - 1) or nslots > block_width:
        return body_spread(orbitals, potential, fitted, points)
    rows = orbitals.shape[0]
    band = lax.axis_index("band")
    total_orbitals = block_width * nbands
    valid_mask = points >= 0
    picks = (points[:, None] == jnp.arange(rows, dtype=points.dtype)[None, :]).astype(jnp.bfloat16)
    rows_b16 = orbitals.astype(jnp.bfloat16)
    selected = jnp.dot(picks, rows_b16, preferred_element_type=jnp.float32).astype(jnp.bfloat16)
    filled = jnp.pad(valid_mask.astype(jnp.bfloat16), (0, block_width - nslots))
    to_band = jnp.concatenate([rows_b16, fitted.reshape(-1, block_width)], 0)
    sent, to_band = lax.optimization_barrier((grid_copies(jnp.concatenate([selected, filled[None]], 0)), to_band))
    got = grid_exchange(sent).reshape(ngroups, nslots + 1, block_width)
    pot = potential[:, None]
    got, orbitals_later = lax.optimization_barrier((got, orbitals))
    swapped = band_hops(to_band)
    rows_b = jnp.concatenate([part[:rows] for part in swapped], 1)
    fitted_got = jnp.stack([part[rows:].reshape(fitted.shape) for part in swapped], 0)
    fitted_all = jnp.take(fitted_got, jnp.arange(nbands, dtype=jnp.int32) ^ band, axis=0)
    fitted_all = fitted_all.reshape(ngroups // 2, 2, nslots, fitted.shape[1])
    coll = jnp.concatenate(band_hops(pair_up(got[:, :nslots])), 1)
    coll, first_pot_psi = lax.optimization_barrier((coll, pot * orbitals_later))
    first_filled = got[:, nslots, :nslots].reshape(ngroups // 2, 2, nslots)[:, 0] > 0
    fitted_all = jnp.where(
        first_filled[:, :, None], fitted_all[:, 0], jnp.flip(fitted_all[:, 1], axis=1)
    ).reshape(-1, fitted.shape[1]).astype(jnp.float32)
    psi = orbitals
    for step in range(ITERS):
        if step:
            at_slots = jnp.dot(picks, psi, preferred_element_type=jnp.float32).astype(jnp.bfloat16)
            high = lax.reduce_precision(sq, exponent_bits=8, mantissa_bits=7)
            rest = sq - high
            middle = lax.reduce_precision(rest, exponent_bits=8, mantissa_bits=7)
            low = lax.reduce_precision(rest - middle, exponent_bits=8, mantissa_bits=7)
            parts = jnp.stack([high, middle, low], 0).astype(jnp.bfloat16)
            got = grid_gather(jnp.concatenate([at_slots, parts], 0)).reshape(ngroups, nslots + 3, block_width)
            sums = got[:, nslots:].astype(jnp.float32)
            total = jnp.sum((sums[:, 0] + sums[:, 1]) + sums[:, 2], axis=0)
            scale = lax.rsqrt(total / (rows * ngroups) + 1e-06)
            coll_own = pair_up((got[:, :nslots].astype(jnp.float32) * scale).astype(jnp.bfloat16))
            psi = psi * scale
            ncoll = coll_own.shape[0]
            swapped = band_hops(jnp.concatenate([coll_own, psi.astype(jnp.bfloat16)], 0))
            coll = jnp.concatenate([part[:ncoll] for part in swapped], 1)
            rows_b = jnp.concatenate([part[ncoll:] for part in swapped], 1)
        proj = None
        for k in range(nbands):
            part = lax.dot_general(
                coll[:, k * block_width:(k + 1) * block_width],
                rows_b[:, k * block_width:(k + 1) * block_width],
                (((1,), (1,)), ((), ())),
                preferred_element_type=jnp.float32,
            )
            part = (part / total_orbitals).astype(jnp.bfloat16).astype(jnp.float32)
            proj = part if proj is None else proj + part
        tile_blocks = (fitted_all * proj).astype(jnp.bfloat16)
        applied = lax.dot_general(
            tile_blocks, coll[:, :block_width], (((0,), (0,)), ((), ())), preferred_element_type=jnp.float32
        )
        pot_psi = first_pot_psi if step == 0 else pot * psi
        psi = psi - 0.25 * (pot_psi - applied)
        sq = jnp.sum(psi * psi, axis=0)
    total = jnp.sum(grid_gather(sq[None]), axis=0)
    return psi * lax.rsqrt(total / (rows * ngroups) + 1e-06)


def body_spread(orbitals, potential, fitted, points):
    rows = orbitals.shape[0]
    block_width = orbitals.shape[1]
    nbands = lax.axis_size("band")
    ngroups = lax.axis_size("grid")
    total_orbitals = block_width * nbands
    valid_mask = points >= 0
    safe_idx = jnp.where(valid_mask, points, 0)
    psi = orbitals
    for step in range(ITERS):
        orbital_block = psi.astype(jnp.bfloat16)
        selected_points = jnp.where(
            valid_mask[:, None], orbital_block[safe_idx], jnp.zeros((), jnp.bfloat16)
        )
        collocation_matrix = lax.all_gather(selected_points, "grid", axis=0, tiled=True)
        product = lax.dot_general(
            collocation_matrix,
            orbital_block,
            (((1,), (1,)), ((), ())),
            preferred_element_type=jnp.float32,
        )
        proj = lax.psum_scatter(
            (product / total_orbitals).astype(jnp.bfloat16), "band", scatter_dimension=0, tiled=True
        ).astype(jnp.float32)
        tile_blocks = (fitted.astype(jnp.float32) * proj).astype(jnp.bfloat16)
        orbitals_at_slots = lax.all_to_all(
            collocation_matrix, "band", split_axis=0, concat_axis=1, tiled=True
        )
        partial_value = lax.dot_general(
            tile_blocks,
            orbitals_at_slots,
            (((0,), (0,)), ((), ())),
            preferred_element_type=jnp.float32,
        )
        applied = lax.psum_scatter(
            partial_value.astype(jnp.bfloat16), "band", scatter_dimension=1, tiled=True
        ).astype(jnp.float32)
        fresh = psi - 0.25 * (potential[:, None] * psi - applied)
        squares = lax.psum(jnp.sum(fresh * fresh, axis=0), "grid")
        psi = fresh * lax.rsqrt(squares / (rows * ngroups) + 1e-06)
    return psi


def solution(mesh):
    in_specs = (P("grid", "band"), P("grid"), P("band", "grid"), P("grid"))
    out_specs = P("grid", "band")
    return jax.shard_map(body, mesh=mesh, in_specs=in_specs, out_specs=out_specs, check_vma=False)
```

```python
import jax
import jax.numpy as jnp
from jax import lax
from jax.sharding import PartitionSpec as P

ITERS = 2


def grid_copies(x):
    ngroups = lax.axis_size("grid")
    return jnp.broadcast_to(x[None], (ngroups,) + x.shape)


def grid_exchange(sent):
    got = lax.all_to_all(sent, "grid", 0, 0, tiled=True)
    return got.reshape((sent.shape[0] * sent.shape[1],) + sent.shape[2:])


def grid_gather(x):
    return grid_exchange(grid_copies(x))


def band_swap(x):
    nbands = lax.axis_size("band")
    got = [x]
    for k in range(1, nbands):
        got.append(lax.ppermute(x, "band", [(i, i ^ k) for i in range(nbands)]))
    return got


def pair_up(slots):
    ngroups, nslots = slots.shape[:2]
    pairs = slots.reshape((ngroups // 2, 2) + slots.shape[1:])
    return (pairs[:, 0] + jnp.flip(pairs[:, 1], axis=1)).reshape((ngroups // 2 * nslots,) + slots.shape[2:])


def band_hops(x):
    nbands = lax.axis_size("band")
    held = {0: x}
    bit = nbands // 2
    while bit:
        keys = sorted(held)
        got = lax.ppermute(jnp.concatenate([held[k] for k in keys], 0), "band", [(i, i ^ bit) for i in range(nbands)])
        for n, k in enumerate(keys):
            held[k ^ bit] = got[n * x.shape[0]:(n + 1) * x.shape[0]]
        bit //= 2
    return [held[k] for k in range(nbands)]


def body(orbitals, potential, fitted, points):
    ngroups = lax.axis_size("grid")
    nbands = lax.axis_size("band")
    nslots = points.shape[0]
    block_width = orbitals.shape[1]
    if ngroups > 8 or ngroups % 2 or nbands & (nbands - 1) or nslots > block_width:
        return body_spread(orbitals, potential, fitted, points)
    rows = orbitals.shape[0]
    band = lax.axis_index("band")
    total_orbitals = block_width * nbands
    valid_mask = points >= 0
    picks = (points[:, None] == jnp.arange(rows, dtype=points.dtype)[None, :]).astype(jnp.bfloat16)
    rows_b16 = orbitals.astype(jnp.bfloat16)
    selected = jnp.dot(picks, rows_b16, preferred_element_type=jnp.float32).astype(jnp.bfloat16)
    filled = jnp.pad(valid_mask.astype(jnp.bfloat16), (0, block_width - nslots))
    to_band = jnp.concatenate([rows_b16, fitted.reshape(-1, block_width)], 0)
    sent, to_band = lax.optimization_barrier((grid_copies(jnp.concatenate([selected, filled[None]], 0)), to_band))
    got = grid_exchange(sent).reshape(ngroups, nslots + 1, block_width)
    pot = potential[:, None]
    got, orbitals_later = lax.optimization_barrier((got, orbitals))
    nband_rows = to_band.shape[0]
    across = lax.ppermute(to_band, "band", [(i, i ^ 2) for i in range(nbands)]) if nbands == 4 else None
    paired = pair_up(got[:, :nslots])
    if nbands == 4:
        paired, across = lax.optimization_barrier((paired, across))
        on_chip = lax.ppermute(jnp.concatenate([to_band, across], 0), "band", [(i, i ^ 1) for i in range(nbands)])
        swapped = [to_band, on_chip[:nband_rows], across, on_chip[nband_rows:]]
    else:
        swapped = band_hops(to_band)
    rows_b = jnp.concatenate([part[:rows] for part in swapped], 1)
    fitted_got = jnp.stack([part[rows:].reshape(fitted.shape) for part in swapped], 0)
    fitted_all = jnp.take(fitted_got, jnp.arange(nbands, dtype=jnp.int32) ^ band, axis=0)
    fitted_all = fitted_all.reshape(ngroups // 2, 2, nslots, fitted.shape[1])
    coll = jnp.concatenate(band_hops(paired), 1)
    coll, first_pot_psi = lax.optimization_barrier((coll, pot * orbitals_later))
    first_filled = got[:, nslots, :nslots].reshape(ngroups // 2, 2, nslots)[:, 0] > 0
    fitted_all = jnp.where(
        first_filled[:, :, None], fitted_all[:, 0], jnp.flip(fitted_all[:, 1], axis=1)
    ).reshape(-1, fitted.shape[1]).astype(jnp.float32)
    psi = orbitals
    for step in range(ITERS):
        if step:
            at_slots = jnp.dot(picks, psi, preferred_element_type=jnp.float32).astype(jnp.bfloat16)
            high = lax.reduce_precision(sq, exponent_bits=8, mantissa_bits=7)
            rest = sq - high
            middle = lax.reduce_precision(rest, exponent_bits=8, mantissa_bits=7)
            low = lax.reduce_precision(rest - middle, exponent_bits=8, mantissa_bits=7)
            parts = jnp.stack([high, middle, low], 0).astype(jnp.bfloat16)
            got = grid_gather(jnp.concatenate([at_slots, parts], 0)).reshape(ngroups, nslots + 3, block_width)
            sums = got[:, nslots:].astype(jnp.float32)
            total = jnp.sum((sums[:, 0] + sums[:, 1]) + sums[:, 2], axis=0)
            scale = lax.rsqrt(total / (rows * ngroups) + 1e-06)
            coll_own = pair_up((got[:, :nslots].astype(jnp.float32) * scale).astype(jnp.bfloat16))
            psi = psi * scale
            ncoll = coll_own.shape[0]
            swapped = band_hops(jnp.concatenate([coll_own, psi.astype(jnp.bfloat16)], 0))
            coll = jnp.concatenate([part[:ncoll] for part in swapped], 1)
            rows_b = jnp.concatenate([part[ncoll:] for part in swapped], 1)
        proj = None
        for k in range(nbands):
            part = lax.dot_general(
                coll[:, k * block_width:(k + 1) * block_width],
                rows_b[:, k * block_width:(k + 1) * block_width],
                (((1,), (1,)), ((), ())),
                preferred_element_type=jnp.float32,
            )
            part = (part / total_orbitals).astype(jnp.bfloat16).astype(jnp.float32)
            proj = part if proj is None else proj + part
        tile_blocks = (fitted_all * proj).astype(jnp.bfloat16)
        applied = lax.dot_general(
            tile_blocks, coll[:, :block_width], (((0,), (0,)), ((), ())), preferred_element_type=jnp.float32
        )
        pot_psi = first_pot_psi if step == 0 else pot * psi
        psi = psi - 0.25 * (pot_psi - applied)
        sq = jnp.sum(psi * psi, axis=0)
    total = jnp.sum(grid_gather(sq[None]), axis=0)
    return psi * lax.rsqrt(total / (rows * ngroups) + 1e-06)


def body_spread(orbitals, potential, fitted, points):
    rows = orbitals.shape[0]
    block_width = orbitals.shape[1]
    nbands = lax.axis_size("band")
    ngroups = lax.axis_size("grid")
    total_orbitals = block_width * nbands
    valid_mask = points >= 0
    safe_idx = jnp.where(valid_mask, points, 0)
    psi = orbitals
    for step in range(ITERS):
        orbital_block = psi.astype(jnp.bfloat16)
        selected_points = jnp.where(
            valid_mask[:, None], orbital_block[safe_idx], jnp.zeros((), jnp.bfloat16)
        )
        collocation_matrix = lax.all_gather(selected_points, "grid", axis=0, tiled=True)
        product = lax.dot_general(
            collocation_matrix,
            orbital_block,
            (((1,), (1,)), ((), ())),
            preferred_element_type=jnp.float32,
        )
        proj = lax.psum_scatter(
            (product / total_orbitals).astype(jnp.bfloat16), "band", scatter_dimension=0, tiled=True
        ).astype(jnp.float32)
        tile_blocks = (fitted.astype(jnp.float32) * proj).astype(jnp.bfloat16)
        orbitals_at_slots = lax.all_to_all(
            collocation_matrix, "band", split_axis=0, concat_axis=1, tiled=True
        )
        partial_value = lax.dot_general(
            tile_blocks,
            orbitals_at_slots,
            (((0,), (0,)), ((), ())),
            preferred_element_type=jnp.float32,
        )
        applied = lax.psum_scatter(
            partial_value.astype(jnp.bfloat16), "band", scatter_dimension=1, tiled=True
        ).astype(jnp.float32)
        fresh = psi - 0.25 * (potential[:, None] * psi - applied)
        squares = lax.psum(jnp.sum(fresh * fresh, axis=0), "grid")
        psi = fresh * lax.rsqrt(squares / (rows * ngroups) + 1e-06)
    return psi


def solution(mesh):
    in_specs = (P("grid", "band"), P("grid"), P("band", "grid"), P("grid"))
    out_specs = P("grid", "band")
    return jax.shard_map(body, mesh=mesh, in_specs=in_specs, out_specs=out_specs, check_vma=False)
```

```python
import jax
import jax.numpy as jnp
from jax import lax
from jax.sharding import PartitionSpec as P

ITERS = 2


def grid_copies(x):
    ngroups = lax.axis_size("grid")
    return jnp.broadcast_to(x[None], (ngroups,) + x.shape)


def grid_exchange(sent):
    got = lax.all_to_all(sent, "grid", 0, 0, tiled=True)
    return got.reshape((sent.shape[0] * sent.shape[1],) + sent.shape[2:])


def grid_gather(x):
    return grid_exchange(grid_copies(x))


def band_swap(x):
    nbands = lax.axis_size("band")
    got = [x]
    for k in range(1, nbands):
        got.append(lax.ppermute(x, "band", [(i, i ^ k) for i in range(nbands)]))
    return got


def pair_up(slots):
    ngroups, nslots = slots.shape[:2]
    pairs = slots.reshape((ngroups // 2, 2) + slots.shape[1:])
    return (pairs[:, 0] + jnp.flip(pairs[:, 1], axis=1)).reshape((ngroups // 2 * nslots,) + slots.shape[2:])


def band_hops(x):
    nbands = lax.axis_size("band")
    held = {0: x}
    bit = nbands // 2
    while bit:
        keys = sorted(held)
        got = lax.ppermute(jnp.concatenate([held[k] for k in keys], 0), "band", [(i, i ^ bit) for i in range(nbands)])
        for n, k in enumerate(keys):
            held[k ^ bit] = got[n * x.shape[0]:(n + 1) * x.shape[0]]
        bit //= 2
    return [held[k] for k in range(nbands)]


def body(orbitals, potential, fitted, points):
    ngroups = lax.axis_size("grid")
    nbands = lax.axis_size("band")
    nslots = points.shape[0]
    block_width = orbitals.shape[1]
    if ngroups > 8 or ngroups % 2 or nbands & (nbands - 1) or nslots > block_width:
        return body_spread(orbitals, potential, fitted, points)
    rows = orbitals.shape[0]
    band = lax.axis_index("band")
    total_orbitals = block_width * nbands
    picks = (points[:, None] == jnp.arange(rows, dtype=points.dtype)[None, :]).astype(jnp.bfloat16)
    rows_b16 = orbitals.astype(jnp.bfloat16)
    selected = jnp.dot(picks, rows_b16, preferred_element_type=jnp.float32).astype(jnp.bfloat16)
    filled = lax.dot_general(
        jnp.ones((1, rows), jnp.bfloat16), picks, (((1,), (1,)), ((), ())), preferred_element_type=jnp.float32
    ).astype(jnp.bfloat16)
    filled = jnp.pad(filled, ((0, 0), (0, block_width - nslots)))
    to_band = jnp.concatenate([rows_b16, fitted.reshape(-1, block_width)], 0)
    sent, to_band = lax.optimization_barrier((grid_copies(jnp.concatenate([selected, filled], 0)), to_band))
    got = grid_exchange(sent).reshape(ngroups, nslots + 1, block_width)
    pot = potential[:, None]
    got, orbitals_later = lax.optimization_barrier((got, orbitals))
    swapped = band_hops(to_band)
    rows_b = jnp.concatenate([part[:rows] for part in swapped], 1)
    fitted_got = jnp.stack([part[rows:].reshape(fitted.shape) for part in swapped], 0)
    fitted_all = jnp.take(fitted_got, jnp.arange(nbands, dtype=jnp.int32) ^ band, axis=0)
    fitted_all = fitted_all.reshape(ngroups // 2, 2, nslots, fitted.shape[1])
    coll = jnp.concatenate(band_hops(pair_up(got[:, :nslots])), 1)
    coll, first_pot_psi = lax.optimization_barrier((coll, pot * orbitals_later))
    first_filled = got[:, nslots, :nslots].reshape(ngroups // 2, 2, nslots)[:, 0] > 0
    fitted_all = jnp.where(
        first_filled[:, :, None], fitted_all[:, 0], jnp.flip(fitted_all[:, 1], axis=1)
    ).reshape(-1, fitted.shape[1]).astype(jnp.float32)
    psi = orbitals
    for step in range(ITERS):
        if step:
            at_slots = jnp.dot(picks, psi, preferred_element_type=jnp.float32).astype(jnp.bfloat16)
            high = lax.reduce_precision(sq, exponent_bits=8, mantissa_bits=7)
            rest = sq - high
            middle = lax.reduce_precision(rest, exponent_bits=8, mantissa_bits=7)
            low = lax.reduce_precision(rest - middle, exponent_bits=8, mantissa_bits=7)
            parts = jnp.stack([high, middle, low], 0).astype(jnp.bfloat16)
            got = grid_gather(jnp.concatenate([at_slots, parts], 0)).reshape(ngroups, nslots + 3, block_width)
            sums = got[:, nslots:].astype(jnp.float32)
            total = jnp.sum((sums[:, 0] + sums[:, 1]) + sums[:, 2], axis=0)
            scale = lax.rsqrt(total / (rows * ngroups) + 1e-06)
            coll_own = pair_up((got[:, :nslots].astype(jnp.float32) * scale).astype(jnp.bfloat16))
            psi = psi * scale
            ncoll = coll_own.shape[0]
            swapped = band_hops(jnp.concatenate([coll_own, psi.astype(jnp.bfloat16)], 0))
            coll = jnp.concatenate([part[:ncoll] for part in swapped], 1)
            rows_b = jnp.concatenate([part[ncoll:] for part in swapped], 1)
        proj = None
        for k in range(nbands):
            part = lax.dot_general(
                coll[:, k * block_width:(k + 1) * block_width],
                rows_b[:, k * block_width:(k + 1) * block_width],
                (((1,), (1,)), ((), ())),
                preferred_element_type=jnp.float32,
            )
            part = (part / total_orbitals).astype(jnp.bfloat16).astype(jnp.float32)
            proj = part if proj is None else proj + part
        tile_blocks = (fitted_all * proj).astype(jnp.bfloat16)
        applied = lax.dot_general(
            tile_blocks, coll[:, :block_width], (((0,), (0,)), ((), ())), preferred_element_type=jnp.float32
        )
        pot_psi = first_pot_psi if step == 0 else pot * psi
        psi = psi - 0.25 * (pot_psi - applied)
        sq = jnp.sum(psi * psi, axis=0)
    total = jnp.sum(grid_gather(sq[None]), axis=0)
    return psi * lax.rsqrt(total / (rows * ngroups) + 1e-06)


def body_spread(orbitals, potential, fitted, points):
    rows = orbitals.shape[0]
    block_width = orbitals.shape[1]
    nbands = lax.axis_size("band")
    ngroups = lax.axis_size("grid")
    total_orbitals = block_width * nbands
    valid_mask = points >= 0
    safe_idx = jnp.where(valid_mask, points, 0)
    psi = orbitals
    for step in range(ITERS):
        orbital_block = psi.astype(jnp.bfloat16)
        selected_points = jnp.where(
            valid_mask[:, None], orbital_block[safe_idx], jnp.zeros((), jnp.bfloat16)
        )
        collocation_matrix = lax.all_gather(selected_points, "grid", axis=0, tiled=True)
        product = lax.dot_general(
            collocation_matrix,
            orbital_block,
            (((1,), (1,)), ((), ())),
            preferred_element_type=jnp.float32,
        )
        proj = lax.psum_scatter(
            (product / total_orbitals).astype(jnp.bfloat16), "band", scatter_dimension=0, tiled=True
        ).astype(jnp.float32)
        tile_blocks = (fitted.astype(jnp.float32) * proj).astype(jnp.bfloat16)
        orbitals_at_slots = lax.all_to_all(
            collocation_matrix, "band", split_axis=0, concat_axis=1, tiled=True
        )
        partial_value = lax.dot_general(
            tile_blocks,
            orbitals_at_slots,
            (((0,), (0,)), ((), ())),
            preferred_element_type=jnp.float32,
        )
        applied = lax.psum_scatter(
            partial_value.astype(jnp.bfloat16), "band", scatter_dimension=1, tiled=True
        ).astype(jnp.float32)
        fresh = psi - 0.25 * (potential[:, None] * psi - applied)
        squares = lax.psum(jnp.sum(fresh * fresh, axis=0), "grid")
        psi = fresh * lax.rsqrt(squares / (rows * ngroups) + 1e-06)
    return psi


def solution(mesh):
    in_specs = (P("grid", "band"), P("grid"), P("band", "grid"), P("grid"))
    out_specs = P("grid", "band")
    return jax.shard_map(body, mesh=mesh, in_specs=in_specs, out_specs=out_specs, check_vma=False)
```

```python
import jax
import jax.numpy as jnp
from jax import lax
from jax.sharding import PartitionSpec as P

ITERS = 2


def grid_copies(x):
    ngroups = lax.axis_size("grid")
    return jnp.broadcast_to(x[None], (ngroups,) + x.shape)


def grid_exchange(sent):
    got = lax.all_to_all(sent, "grid", 0, 0, tiled=True)
    return got.reshape((sent.shape[0] * sent.shape[1],) + sent.shape[2:])


def grid_gather(x):
    return grid_exchange(grid_copies(x))


def band_swap(x):
    nbands = lax.axis_size("band")
    got = [x]
    for k in range(1, nbands):
        got.append(lax.ppermute(x, "band", [(i, i ^ k) for i in range(nbands)]))
    return got


def pair_up(slots):
    ngroups, nslots = slots.shape[:2]
    pairs = slots.reshape((ngroups // 2, 2) + slots.shape[1:])
    return (pairs[:, 0] + jnp.flip(pairs[:, 1], axis=1)).reshape((ngroups // 2 * nslots,) + slots.shape[2:])


def band_hops(x):
    nbands = lax.axis_size("band")
    held = {0: x}
    bit = nbands // 2
    while bit:
        keys = sorted(held)
        got = lax.ppermute(jnp.concatenate([held[k] for k in keys], 0), "band", [(i, i ^ bit) for i in range(nbands)])
        for n, k in enumerate(keys):
            held[k ^ bit] = got[n * x.shape[0]:(n + 1) * x.shape[0]]
        bit //= 2
    return [held[k] for k in range(nbands)]


def body(orbitals, potential, fitted, points):
    ngroups = lax.axis_size("grid")
    nbands = lax.axis_size("band")
    nslots = points.shape[0]
    block_width = orbitals.shape[1]
    if ngroups > 8 or ngroups % 2 or nbands & (nbands - 1) or nslots > block_width:
        return body_spread(orbitals, potential, fitted, points)
    rows = orbitals.shape[0]
    band = lax.axis_index("band")
    total_orbitals = block_width * nbands
    valid_mask = points >= 0
    picks = (points[:, None] == jnp.arange(rows, dtype=points.dtype)[None, :]).astype(jnp.bfloat16)
    rows_b16 = orbitals.astype(jnp.bfloat16)
    selected = jnp.dot(picks, rows_b16, preferred_element_type=jnp.float32).astype(jnp.bfloat16)
    filled = jnp.pad(valid_mask.astype(jnp.bfloat16), (0, block_width - nslots))
    to_band = jnp.concatenate([rows_b16, fitted.reshape(-1, block_width)], 0)
    sent, to_band = lax.optimization_barrier((grid_copies(jnp.concatenate([selected, filled[None]], 0)), to_band))
    got = grid_exchange(sent).reshape(ngroups, nslots + 1, block_width)
    pot = potential[:, None]
    got, orbitals_later = lax.optimization_barrier((got, orbitals))
    swapped = band_swap(to_band)
    rows_b = jnp.concatenate([part[:rows] for part in swapped], 1)
    fitted_got = jnp.stack([part[rows:].reshape(fitted.shape) for part in swapped], 0)
    fitted_all = jnp.take(fitted_got, jnp.arange(nbands, dtype=jnp.int32) ^ band, axis=0)
    fitted_all = fitted_all.reshape(ngroups // 2, 2, nslots, fitted.shape[1])
    coll = jnp.concatenate(band_hops(pair_up(got[:, :nslots])), 1)
    coll, first_pot_psi = lax.optimization_barrier((coll, pot * orbitals_later))
    first_filled = got[:, nslots, :nslots].reshape(ngroups // 2, 2, nslots)[:, 0] > 0
    fitted_all = jnp.where(
        first_filled[:, :, None], fitted_all[:, 0], jnp.flip(fitted_all[:, 1], axis=1)
    ).reshape(-1, fitted.shape[1]).astype(jnp.float32)
    psi = orbitals
    for step in range(ITERS):
        if step:
            at_slots = jnp.dot(picks, psi, preferred_element_type=jnp.float32).astype(jnp.bfloat16)
            high = lax.reduce_precision(sq, exponent_bits=8, mantissa_bits=7)
            rest = sq - high
            middle = lax.reduce_precision(rest, exponent_bits=8, mantissa_bits=7)
            low = lax.reduce_precision(rest - middle, exponent_bits=8, mantissa_bits=7)
            parts = jnp.stack([high, middle, low], 0).astype(jnp.bfloat16)
            got = grid_gather(jnp.concatenate([at_slots, parts], 0)).reshape(ngroups, nslots + 3, block_width)
            sums = got[:, nslots:].astype(jnp.float32)
            total = jnp.sum((sums[:, 0] + sums[:, 1]) + sums[:, 2], axis=0)
            scale = lax.rsqrt(total / (rows * ngroups) + 1e-06)
            coll_own = pair_up((got[:, :nslots].astype(jnp.float32) * scale).astype(jnp.bfloat16))
            psi = psi * scale
            ncoll = coll_own.shape[0]
            swapped = band_hops(jnp.concatenate([coll_own, psi.astype(jnp.bfloat16)], 0))
            coll = jnp.concatenate([part[:ncoll] for part in swapped], 1)
            rows_b = jnp.concatenate([part[ncoll:] for part in swapped], 1)
        proj = None
        for k in range(nbands):
            part = lax.dot_general(
                coll[:, k * block_width:(k + 1) * block_width],
                rows_b[:, k * block_width:(k + 1) * block_width],
                (((1,), (1,)), ((), ())),
                preferred_element_type=jnp.float32,
            )
            part = (part / total_orbitals).astype(jnp.bfloat16).astype(jnp.float32)
            proj = part if proj is None else proj + part
        tile_blocks = (fitted_all * proj).astype(jnp.bfloat16)
        applied = lax.dot_general(
            tile_blocks, coll[:, :block_width], (((0,), (0,)), ((), ())), preferred_element_type=jnp.float32
        )
        pot_psi = first_pot_psi if step == 0 else pot * psi
        psi = psi - 0.25 * (pot_psi - applied)
        sq = jnp.sum(psi * psi, axis=0)
    total = jnp.sum(grid_gather(sq[None]), axis=0)
    return psi * lax.rsqrt(total / (rows * ngroups) + 1e-06)


def body_spread(orbitals, potential, fitted, points):
    rows = orbitals.shape[0]
    block_width = orbitals.shape[1]
    nbands = lax.axis_size("band")
    ngroups = lax.axis_size("grid")
    total_orbitals = block_width * nbands
    valid_mask = points >= 0
    safe_idx = jnp.where(valid_mask, points, 0)
    psi = orbitals
    for step in range(ITERS):
        orbital_block = psi.astype(jnp.bfloat16)
        selected_points = jnp.where(
            valid_mask[:, None], orbital_block[safe_idx], jnp.zeros((), jnp.bfloat16)
        )
        collocation_matrix = lax.all_gather(selected_points, "grid", axis=0, tiled=True)
        product = lax.dot_general(
            collocation_matrix,
            orbital_block,
            (((1,), (1,)), ((), ())),
            preferred_element_type=jnp.float32,
        )
        proj = lax.psum_scatter(
            (product / total_orbitals).astype(jnp.bfloat16), "band", scatter_dimension=0, tiled=True
        ).astype(jnp.float32)
        tile_blocks = (fitted.astype(jnp.float32) * proj).astype(jnp.bfloat16)
        orbitals_at_slots = lax.all_to_all(
            collocation_matrix, "band", split_axis=0, concat_axis=1, tiled=True
        )
        partial_value = lax.dot_general(
            tile_blocks,
            orbitals_at_slots,
            (((0,), (0,)), ((), ())),
            preferred_element_type=jnp.float32,
        )
        applied = lax.psum_scatter(
            partial_value.astype(jnp.bfloat16), "band", scatter_dimension=1, tiled=True
        ).astype(jnp.float32)
        fresh = psi - 0.25 * (potential[:, None] * psi - applied)
        squares = lax.psum(jnp.sum(fresh * fresh, axis=0), "grid")
        psi = fresh * lax.rsqrt(squares / (rows * ngroups) + 1e-06)
    return psi


def solution(mesh):
    in_specs = (P("grid", "band"), P("grid"), P("band", "grid"), P("grid"))
    out_specs = P("grid", "band")
    return jax.shard_map(body, mesh=mesh, in_specs=in_specs, out_specs=out_specs, check_vma=False)
```

```python
import jax
import jax.numpy as jnp
from jax import lax
from jax.sharding import PartitionSpec as P

ITERS = 2


def grid_copies(x):
    ngroups = lax.axis_size("grid")
    return jnp.broadcast_to(x[None], (ngroups,) + x.shape)


def grid_exchange(sent):
    got = lax.all_to_all(sent, "grid", 0, 0, tiled=True)
    return got.reshape((sent.shape[0] * sent.shape[1],) + sent.shape[2:])


def grid_gather(x):
    return grid_exchange(grid_copies(x))


def band_swap(x):
    nbands = lax.axis_size("band")
    got = [x]
    for k in range(1, nbands):
        got.append(lax.ppermute(x, "band", [(i, i ^ k) for i in range(nbands)]))
    return got


def pair_up(slots):
    ngroups, nslots = slots.shape[:2]
    pairs = slots.reshape((ngroups // 2, 2) + slots.shape[1:])
    return (pairs[:, 0] + jnp.flip(pairs[:, 1], axis=1)).reshape((ngroups // 2 * nslots,) + slots.shape[2:])


def band_hops(x):
    nbands = lax.axis_size("band")
    held = {0: x}
    bit = nbands // 2
    while bit:
        keys = sorted(held)
        got = lax.ppermute(jnp.concatenate([held[k] for k in keys], 0), "band", [(i, i ^ bit) for i in range(nbands)])
        for n, k in enumerate(keys):
            held[k ^ bit] = got[n * x.shape[0]:(n + 1) * x.shape[0]]
        bit //= 2
    return [held[k] for k in range(nbands)]


def body(orbitals, potential, fitted, points):
    ngroups = lax.axis_size("grid")
    nbands = lax.axis_size("band")
    nslots = points.shape[0]
    block_width = orbitals.shape[1]
    if ngroups > 8 or ngroups % 2 or nbands & (nbands - 1) or nslots > block_width:
        return body_spread(orbitals, potential, fitted, points)
    rows = orbitals.shape[0]
    band = lax.axis_index("band")
    total_orbitals = block_width * nbands
    valid_mask = points >= 0
    picks = (points[:, None] == jnp.arange(rows, dtype=points.dtype)[None, :]).astype(jnp.bfloat16)
    rows_b16 = orbitals.astype(jnp.bfloat16)
    selected = jnp.dot(picks, rows_b16, preferred_element_type=jnp.float32).astype(jnp.bfloat16)
    filled = jnp.pad(valid_mask.astype(jnp.bfloat16), (0, block_width - nslots))
    to_band = jnp.concatenate([rows_b16, fitted.reshape(-1, block_width)], 0)
    sent, to_band = lax.optimization_barrier((grid_copies(jnp.concatenate([selected, filled[None]], 0)), to_band))
    got = grid_exchange(sent).reshape(ngroups, nslots + 1, block_width)
    pot = potential[:, None]
    got, orbitals_later = lax.optimization_barrier((got, orbitals))
    swapped = band_hops(to_band)
    rows_b = jnp.concatenate([part[:rows] for part in swapped], 1)
    fitted_got = jnp.stack([part[rows:].reshape(fitted.shape) for part in swapped], 0)
    ordered = []
    for j in range(nbands):
        pick = fitted_got[nbands - 1]
        for k in range(nbands - 2, -1, -1):
            pick = jnp.where(band == (j ^ k), fitted_got[k], pick)
        ordered.append(pick)
    fitted_all = jnp.stack(ordered, 0).reshape(ngroups // 2, 2, nslots, fitted.shape[1])
    coll = jnp.concatenate(band_hops(pair_up(got[:, :nslots])), 1)
    coll, first_pot_psi = lax.optimization_barrier((coll, pot * orbitals_later))
    first_filled = got[:, nslots, :nslots].reshape(ngroups // 2, 2, nslots)[:, 0] > 0
    fitted_all = jnp.where(
        first_filled[:, :, None], fitted_all[:, 0], jnp.flip(fitted_all[:, 1], axis=1)
    ).reshape(-1, fitted.shape[1]).astype(jnp.float32)
    psi = orbitals
    for step in range(ITERS):
        if step:
            at_slots = jnp.dot(picks, psi, preferred_element_type=jnp.float32).astype(jnp.bfloat16)
            high = lax.reduce_precision(sq, exponent_bits=8, mantissa_bits=7)
            rest = sq - high
            middle = lax.reduce_precision(rest, exponent_bits=8, mantissa_bits=7)
            low = lax.reduce_precision(rest - middle, exponent_bits=8, mantissa_bits=7)
            parts = jnp.stack([high, middle, low], 0).astype(jnp.bfloat16)
            got = grid_gather(jnp.concatenate([at_slots, parts], 0)).reshape(ngroups, nslots + 3, block_width)
            sums = got[:, nslots:].astype(jnp.float32)
            total = jnp.sum((sums[:, 0] + sums[:, 1]) + sums[:, 2], axis=0)
            scale = lax.rsqrt(total / (rows * ngroups) + 1e-06)
            coll_own = pair_up((got[:, :nslots].astype(jnp.float32) * scale).astype(jnp.bfloat16))
            psi = psi * scale
            ncoll = coll_own.shape[0]
            swapped = band_hops(jnp.concatenate([coll_own, psi.astype(jnp.bfloat16)], 0))
            coll = jnp.concatenate([part[:ncoll] for part in swapped], 1)
            rows_b = jnp.concatenate([part[ncoll:] for part in swapped], 1)
        proj = None
        for k in range(nbands):
            part = lax.dot_general(
                coll[:, k * block_width:(k + 1) * block_width],
                rows_b[:, k * block_width:(k + 1) * block_width],
                (((1,), (1,)), ((), ())),
                preferred_element_type=jnp.float32,
            )
            part = (part / total_orbitals).astype(jnp.bfloat16).astype(jnp.float32)
            proj = part if proj is None else proj + part
        tile_blocks = (fitted_all * proj).astype(jnp.bfloat16)
        applied = lax.dot_general(
            tile_blocks, coll[:, :block_width], (((0,), (0,)), ((), ())), preferred_element_type=jnp.float32
        )
        pot_psi = first_pot_psi if step == 0 else pot * psi
        psi = psi - 0.25 * (pot_psi - applied)
        sq = jnp.sum(psi * psi, axis=0)
    total = jnp.sum(grid_gather(sq[None]), axis=0)
    return psi * lax.rsqrt(total / (rows * ngroups) + 1e-06)


def body_spread(orbitals, potential, fitted, points):
    rows = orbitals.shape[0]
    block_width = orbitals.shape[1]
    nbands = lax.axis_size("band")
    ngroups = lax.axis_size("grid")
    total_orbitals = block_width * nbands
    valid_mask = points >= 0
    safe_idx = jnp.where(valid_mask, points, 0)
    psi = orbitals
    for step in range(ITERS):
        orbital_block = psi.astype(jnp.bfloat16)
        selected_points = jnp.where(
            valid_mask[:, None], orbital_block[safe_idx], jnp.zeros((), jnp.bfloat16)
        )
        collocation_matrix = lax.all_gather(selected_points, "grid", axis=0, tiled=True)
        product = lax.dot_general(
            collocation_matrix,
            orbital_block,
            (((1,), (1,)), ((), ())),
            preferred_element_type=jnp.float32,
        )
        proj = lax.psum_scatter(
            (product / total_orbitals).astype(jnp.bfloat16), "band", scatter_dimension=0, tiled=True
        ).astype(jnp.float32)
        tile_blocks = (fitted.astype(jnp.float32) * proj).astype(jnp.bfloat16)
        orbitals_at_slots = lax.all_to_all(
            collocation_matrix, "band", split_axis=0, concat_axis=1, tiled=True
        )
        partial_value = lax.dot_general(
            tile_blocks,
            orbitals_at_slots,
            (((0,), (0,)), ((), ())),
            preferred_element_type=jnp.float32,
        )
        applied = lax.psum_scatter(
            partial_value.astype(jnp.bfloat16), "band", scatter_dimension=1, tiled=True
        ).astype(jnp.float32)
        fresh = psi - 0.25 * (potential[:, None] * psi - applied)
        squares = lax.psum(jnp.sum(fresh * fresh, axis=0), "grid")
        psi = fresh * lax.rsqrt(squares / (rows * ngroups) + 1e-06)
    return psi


def solution(mesh):
    in_specs = (P("grid", "band"), P("grid"), P("band", "grid"), P("grid"))
    out_specs = P("grid", "band")
    return jax.shard_map(body, mesh=mesh, in_specs=in_specs, out_specs=out_specs, check_vma=False)
```
